512 devices in a mesh: seq: 128 (over z, y, core), tp: 4 (over x).
Axes of the slice: x: 4, y: 8, z: 8, core: 2. Of those that a mesh axis runs over, the one named last changes fastest.
Arguments:
- hidden_in: bfloat16 [16384, 1536], P('seq'), may hold values from -6 to 6
- w_query: bfloat16 [1536, 1536], P(None, 'tp'), may hold values from -0.625 to 0.625
- key_weight: bfloat16 [1536, 512], P(None, 'tp'), may hold values from -0.625 to 0.625
- value_weight: bfloat16 [1536, 512], P(None, 'tp'), may hold values from -0.15625 to 0.15625
- w_out: bfloat16 [1536, 1536], P('tp'), may hold values from -0.4375 to 0.4375
- cached_prefix_keys: bfloat16 [4096, 512], P('seq', 'tp'), may hold values from -60000 to 60000
- cached_prefix_values: bfloat16 [4096, 512], P('seq', 'tp'), may hold values from -6 to 6
- doc_ids: int32 [128, 128], P('seq'), may hold values from 0 to 3, never falling along the last dimension, each value on 1 to 64 neighbouring positions
- routes: int32 [16384, 8], P(('seq', 'tp')), may hold values from 0 to 31, all different within a row; in each aligned block of 32 rows (0 to 31, 32 to 63, ...) at most 16 rows name the same one
- gate_scores: float32 [16384, 8], P(('seq', 'tp')), may hold values from 0.2 to 1
- expert_in: bfloat16 [128, 1536, 256], P('seq'), may hold values from -0.15625 to 0.15625
- expert_out: bfloat16 [128, 128, 1536], P('seq'), may hold values from -0.25 to 0.25
Outputs:
- attn_proj: bfloat16 [16384, 1536], P(('seq', 'tp'))
- expert_mix: bfloat16 [16384, 1536], P(('seq', 'tp'))
- layer_out: bfloat16 [16384, 1536], P(('seq', 'tp'))
The draws below stay inside these ranges and needn't reach their ends.
Inputs may be any that keep to these rules, and one draw needn't show every extreme that they name: `routes`: within the rows of one device (aligned blocks of 32 tokens) no expert is picked by more than 16 tokens, a bound that some block reaches; every expert is picked somewhere.
All inputs are finite; a program needn't handle non-finite values.
Results may differ from the reference program's by a relative error of at most 0.028.
Values may be sent and summed in bfloat16 or wider, within the bound.
No kernel may reach another device: no remote copies, remote signals or barrier semaphores. Data moves between devices by JAX's collectives and lax.ppermute only.
A program may use at most 64 MiB of HBM per device.

```python
import math
import jax
import jax.numpy as jnp
import numpy as np
from jax import lax

MODEL_WIDTH = 1536
QUERY_HEADS = 24
KEY_VALUE_HEADS = 8
HEAD_WIDTH = 64
FF_E = 512
EXPERTS = 32
TOP = 8
SUFFIX_TOKENS = 128
DOCS_DEV = 4
TOKENS = 16384
PREFIX_TOKENS = 4096
MOE_ROWS = 32
CAP = 16
HPARTS = 4
UNITS = 128
FF_S = 128
N_SEQ = 128
N_TP = 4


def draw_cached_prefix_keys(key, part):
    streams = jax.random.split(key, 3)
    column_list = KEY_VALUE_HEADS * HEAD_WIDTH
    entries = jax.random.normal(streams[0], (PREFIX_TOKENS, column_list), jnp.float32)
    row_scale = jnp.exp(jax.random.uniform(streams[1], (PREFIX_TOKENS, 1), jnp.float32, math.log(4.5), math.log(5.5)))
    col_scale = jnp.exp(jax.random.uniform(streams[2], (1, column_list), jnp.float32, math.log(0.5), math.log(2.0)))
    scaled = entries * row_scale * col_scale
    return scaled.astype(jnp.bfloat16)


def shard_levels(key, shape, pieces, low, top_value):
    factor_of, own = 1.0, jax.random.fold_in(key, 6)
    for dim, parts in pieces:
        heights = jnp.exp(jax.random.uniform(jax.random.fold_in(own, dim), (parts,), jnp.float32, low / len(pieces), top_value / len(pieces)))
        factor_of = factor_of * jnp.repeat(heights, shape[dim] // parts).reshape([-1 if axis == dim else 1 for axis in range(len(shape))])
    return factor_of


def length_profile(number_of, total, limit, lean):
    loads = [(1 << 20) // math.isqrt(grade ** lean) + 1 for grade in range(2, number_of + 1)]
    rest, given = total - limit - (number_of - 1), [1] * (number_of - 1)
    while rest > 0:
        candidates = [i for i in range(number_of - 1) if given[i] < limit]
        pool, remaining = sum([loads[i] for i in candidates]), rest
        for i in candidates:
            more = min(limit - given[i], max(1, remaining * loads[i] // pool), rest)
            given[i] = given[i] + more
            rest = rest - more
    return np.array([limit] + given)


def uneven(rng, amount, total, most, skew):
    if amount == 2:
        one = jax.random.randint(rng, (), max(1, total - most), min(most, total - 1) + 1)
        return jnp.stack([one, total - one])
    tallies = jnp.asarray(length_profile(amount, total, most, skew), jnp.int32)
    twos = (amount - 1) // 2
    donor, sink = tallies[1:1 + 2 * twos:2], tallies[2:2 + 2 * twos:2]
    margin = jnp.minimum(donor - 1, most - sink)
    passed = jax.random.randint(jax.random.fold_in(rng, 1), (twos,), 0, 1 << 20) % (margin + 1)
    tallies = tallies.at[1:1 + 2 * twos:2].set(donor - passed).at[2:2 + 2 * twos:2].set(sink + passed)
    return tallies[jax.random.permutation(jax.random.fold_in(rng, 2), amount)]


def shared_out(rng, own, number, rows, count, top, reach, slope):
    sequence = jax.random.permutation(rng, count)
    packed, common = shares(count, rows * top, reach, slope, True), shares(count, rows * top, reach, slope, False)
    places = jnp.arange(count)

    def named(sizes, offset_by):
        used = int((sizes > 0).sum())
        fixed = max(1, used // 4)
        passed = fixed + (places - fixed + offset_by * (used - fixed)) % max(1, count - fixed)
        return jnp.zeros((count,), jnp.int32).at[sequence[jnp.where(places < fixed, places, passed)]].set(jnp.asarray(sizes, jnp.int32))

    sizes = jnp.where(number % 4 == 0, named(packed, number // 4), named(common, number - number // 4 - 1))
    mixed = jax.random.permutation(jax.random.fold_in(own, 3), count)
    donor, sink = mixed[0:count // 2 * 2:2], mixed[1:count // 2 * 2:2]
    slack = jnp.minimum(sizes[donor] - 1, reach - sizes[sink]) // 2
    slack = jnp.where((donor == sequence[0]) | (sink == sequence[0]) | (sizes[sink] == 0), 0, jnp.maximum(slack, 0))
    passed = jax.random.randint(jax.random.fold_in(own, 4), (count // 2,), 0, 1 << 20) % (slack + 1)
    sizes = sizes.at[donor].add(-passed).at[sink].add(passed)
    items = jnp.searchsorted(jnp.cumsum(sizes), jnp.arange(rows * top), side="right").astype(jnp.int32)
    listing = items.reshape(top, rows).T
    listing = listing[jax.random.permutation(jax.random.fold_in(own, 1), rows)]
    offset_by = jax.random.randint(jax.random.fold_in(own, 2), (rows, 1), 0, top)
    return jnp.take_along_axis(listing, (jnp.arange(top)[None, :] + offset_by) % top, axis=1)


def shares(count, total, most, skew, full):
    loads = [(1 << 20) // math.isqrt(grade ** skew) + 1 for grade in range(1, count + 1)]
    largest = most if full else min(most, max(-(-total // count), total * loads[0] // sum(loads)))
    least = 1 if total - largest >= count - 1 else 0
    holding, rest = [largest] + [least] * (count - 1), total - largest - least * (count - 1)
    while rest > 0:
        free = [i for i in range(1, count) if holding[i] < largest] or [i for i in range(1, count) if holding[i] < most]
        pool, budget = sum([loads[i] for i in free]), rest
        for i in free:
            more = min(most - holding[i], max(1, budget * loads[i] // pool), rest)
            holding[i] = holding[i] + more
            rest = rest - more
    return np.array(holding)


def normal_values(rng, dims, width, most, cuts=(), kind=jnp.bfloat16):
    loudness = shard_levels(rng, dims, cuts, -0.22, 0.18) if cuts else 1.0
    drawn = jax.random.normal(rng, dims, jnp.float32) * width * loudness
    return jnp.minimum(jnp.maximum(drawn, -most), most).astype(kind)


def setup_inputs(seed: int = 0) -> dict:
    keys = jax.random.split(jax.random.key(seed), 13)
    hidden_in = normal_values(keys[0], (TOKENS, MODEL_WIDTH), 1.0, 6.0, ((0, 128),))
    w_query = normal_values(keys[1], (MODEL_WIDTH, QUERY_HEADS * HEAD_WIDTH), (MODEL_WIDTH // 16) ** -0.5, 0.625, ((1, 4),))
    key_weight = normal_values(keys[2], (MODEL_WIDTH, KEY_VALUE_HEADS * HEAD_WIDTH), (MODEL_WIDTH // 16) ** -0.5, 0.625, ((1, 4),))
    value_weight = normal_values(keys[3], (MODEL_WIDTH, KEY_VALUE_HEADS * HEAD_WIDTH), MODEL_WIDTH ** -0.5, 0.15625, ((1, 4),))
    w_out = normal_values(keys[4], (QUERY_HEADS * HEAD_WIDTH, MODEL_WIDTH), (QUERY_HEADS * HEAD_WIDTH // 8) ** -0.5, 0.4375, ((0, 4),))
    cached_prefix_keys = draw_cached_prefix_keys(jax.random.fold_in(keys[12], 71), 0)
    cached_prefix_values = normal_values(keys[6], (PREFIX_TOKENS, KEY_VALUE_HEADS * HEAD_WIDTH), 1.0, 6.0, ((0, 128), (1, 4)))
    doc_ids = jax.vmap(lambda own: jnp.searchsorted(jnp.cumsum(uneven(own, DOCS_DEV, SUFFIX_TOKENS, SUFFIX_TOKENS // 2, 2)), jnp.arange(SUFFIX_TOKENS), side="right"))(jax.random.split(keys[7], N_SEQ)).reshape((N_SEQ, SUFFIX_TOKENS)).astype(jnp.int32)
    routes_keys = jax.random.split(jax.random.fold_in(keys[8], 1), TOKENS // MOE_ROWS)
    routes_turns = jax.random.permutation(jax.random.fold_in(keys[8], 3), TOKENS // MOE_ROWS)
    routes = jax.vmap(lambda own, number: shared_out(jax.random.fold_in(keys[8], 2), own, number, MOE_ROWS, EXPERTS, TOP, CAP, 2))(routes_keys, routes_turns).reshape((TOKENS, TOP))
    gate_scores = jnp.clip(0.2 + 0.8 * jax.random.uniform(keys[9], (TOKENS, TOP), jnp.float32) ** shard_levels(keys[9], (TOKENS, TOP), ((0, 512),), -0.2, 0.2), 0.2, 1.0)
    expert_in = normal_values(keys[10], (UNITS, MODEL_WIDTH, 2 * FF_S), MODEL_WIDTH ** -0.5, 0.15625, ((0, 128),))
    expert_out = normal_values(keys[11], (UNITS, FF_S, MODEL_WIDTH), FF_E ** -0.5, 0.25, ((0, 128),))
    return {"hidden_in": hidden_in, "w_query": w_query, "key_weight": key_weight, "value_weight": value_weight, "w_out": w_out, "cached_prefix_keys": cached_prefix_keys, "cached_prefix_values": cached_prefix_values, "doc_ids": doc_ids, "routes": routes, "gate_scores": gate_scores, "expert_in": expert_in, "expert_out": expert_out}


EPSILON = 1e-06
RESIDUAL = 0.22

def normalize(values):
    values = values.astype(jnp.float32)
    return values * lax.rsqrt(lax.optimization_barrier(jnp.mean(values * values, axis=-1, keepdims=True)) + EPSILON)

def rotary_apply(values, token_positions):
    half_size = values.shape[-1] // 2
    frequency = jnp.exp(-jnp.log(10000.0) * jnp.arange(half_size, dtype=jnp.float32) * 2.0 / values.shape[-1])
    angles = token_positions[:, None] * frequency[None, :]
    cosine = jnp.cos(angles)[:, None, :]
    sine_part = jnp.sin(angles)[:, None, :]
    first_half = values[..., :half_size]
    second = values[..., half_size:]
    return jnp.concatenate([first_half * cosine - second * sine_part, second * cosine + first_half * sine_part], axis=-1)

def rounded_value(values):
    return lax.optimization_barrier(values.astype(jnp.bfloat16)).astype(jnp.float32)

def reference(hidden_in, w_query, key_weight, value_weight, w_out, cached_prefix_keys, cached_prefix_values, doc_ids, routes, gate_scores, expert_in, expert_out):
    group_width = QUERY_HEADS // KEY_VALUE_HEADS
    earlier_keys = cached_prefix_keys.astype(jnp.float32).reshape(PREFIX_TOKENS, KEY_VALUE_HEADS, HEAD_WIDTH)
    earlier_values = cached_prefix_values.astype(jnp.float32).reshape(PREFIX_TOKENS, KEY_VALUE_HEADS, HEAD_WIDTH)

    def attend(block_args):
        block_rows, doc_row = block_args
        row_index = jnp.arange(SUFFIX_TOKENS, dtype=jnp.int32)
        same_doc = doc_row[:, None] == doc_row[None, :]
        doc_start = lax.optimization_barrier(jnp.min(jnp.where(same_doc, row_index[None, :], SUFFIX_TOKENS), axis=1))
        token_positions = (PREFIX_TOKENS + row_index - doc_start).astype(jnp.float32)
        normed_input = normalize(block_rows).astype(jnp.bfloat16)
        query_rows_all = jnp.dot(normed_input, w_query, preferred_element_type=jnp.float32).reshape(SUFFIX_TOKENS, QUERY_HEADS, HEAD_WIDTH)
        query_rows_all = rounded_value(rotary_apply(query_rows_all, token_positions)).reshape(SUFFIX_TOKENS, KEY_VALUE_HEADS, group_width, HEAD_WIDTH)
        fresh_key = jnp.dot(normed_input, key_weight, preferred_element_type=jnp.float32).reshape(SUFFIX_TOKENS, KEY_VALUE_HEADS, HEAD_WIDTH)
        fresh_key = rounded_value(rotary_apply(fresh_key, token_positions))
        fresh_value = rounded_value(jnp.dot(normed_input, value_weight, preferred_element_type=jnp.float32)).reshape(SUFFIX_TOKENS, KEY_VALUE_HEADS, HEAD_WIDTH)
        scores_pre = jnp.einsum('tkgd,pkd->tkgp', query_rows_all, earlier_keys) / HEAD_WIDTH
        scores_own = jnp.einsum('tkgd,skd->tkgs', query_rows_all, fresh_key) / HEAD_WIDTH
        visible = same_doc & (row_index[None, :] <= row_index[:, None])
        scores_own = jnp.where(visible[:, None, None, :], scores_own, -jnp.inf)
        row_top = jnp.maximum(lax.optimization_barrier(jnp.max(scores_pre, axis=-1)), lax.optimization_barrier(jnp.max(scores_own, axis=-1)))
        weights_pre = jnp.exp(scores_pre - row_top[..., None])
        weights_own = jnp.exp(scores_own - row_top[..., None])
        denominator = lax.optimization_barrier(jnp.sum(weights_pre, axis=-1)) + lax.optimization_barrier(jnp.sum(weights_own, axis=-1))
        numerator = jnp.einsum('tkgp,pkd->tkgd', rounded_value(weights_pre), earlier_values)
        numerator = numerator + jnp.einsum('tkgs,skd->tkgd', rounded_value(weights_own), fresh_value)
        return (numerator / denominator[..., None]).astype(jnp.bfloat16).reshape(SUFFIX_TOKENS, QUERY_HEADS * HEAD_WIDTH)
    attended = lax.map(attend, (hidden_in.reshape(N_SEQ, SUFFIX_TOKENS, MODEL_WIDTH), doc_ids)).reshape(TOKENS, QUERY_HEADS * HEAD_WIDTH)
    attn_sum = jnp.dot(attended, w_out, preferred_element_type=jnp.float32)
    residual = hidden_in.astype(jnp.float32) + RESIDUAL * attn_sum
    routed = normalize(residual).astype(jnp.bfloat16)
    slot_limit = N_SEQ * N_TP * CAP
    block_size = math.gcd(512, slot_limit)
    slot_index = jnp.arange(slot_limit, dtype=jnp.int32)

    def expert_step(expert, total):
        hit_mask = routes == expert
        weight = lax.optimization_barrier(jnp.sum(jnp.where(hit_mask, gate_scores, 0.0), axis=1))
        chosen = jnp.any(hit_mask, axis=1)
        chosen_count = jnp.sum(chosen.astype(jnp.int32)).astype(jnp.int32)
        slots = jnp.nonzero(chosen, size=slot_limit, fill_value=0)[0].astype(jnp.int32)
        slot_weight = jnp.where(slot_index < chosen_count, weight[slots], 0.0)
        first_unit = (expert * HPARTS).astype(jnp.int32)
        weight_in = lax.dynamic_slice_in_dim(expert_in, first_unit, HPARTS, 0).astype(jnp.float32)
        weight_back = lax.dynamic_slice_in_dim(expert_out, first_unit, HPARTS, 0).astype(jnp.float32)

        def block_step(step, running):
            begin = (step * block_size).astype(jnp.int32)
            span = lax.dynamic_slice_in_dim(slots, begin, block_size, 0)
            span_weight = lax.dynamic_slice_in_dim(slot_weight, begin, block_size, 0)
            span_rows = routed[span].astype(jnp.float32)
            gate_up = jnp.einsum('rd,pdf->prf', span_rows, weight_in)
            activated = rounded_value(jax.nn.silu(gate_up[..., :FF_S]) * gate_up[..., FF_S:])
            partial_value = rounded_value(jnp.einsum('prf,pfd->prd', activated, weight_back))
            summed = lax.optimization_barrier(jnp.sum(partial_value, axis=0))
            return running.at[span].add(span_weight[:, None] * summed)
        trip_count = (chosen_count + block_size - 1) // block_size
        return lax.fori_loop(0, trip_count, block_step, total)
    expert_sum = lax.fori_loop(0, EXPERTS, expert_step, jnp.zeros((TOKENS, MODEL_WIDTH), jnp.float32))
    layer_out = (residual + RESIDUAL * expert_sum).astype(jnp.bfloat16)
    return (attn_sum.astype(jnp.bfloat16), expert_sum.astype(jnp.bfloat16), layer_out)
```

```python
import jax
import jax.numpy as jnp
from jax import lax
from jax.sharding import Mesh, PartitionSpec as P

HEAD_WIDTH = 64
EXPERTS = 32


SEQ = ("z", "yh", "yl", "c")
EXPERT_AXES = ("z", "yh")
PART_AXES = ("yl", "c")

EPSILON = 1e-06
RESIDUAL = 0.22


def normalize(values):
    values = values.astype(jnp.float32)
    return values * lax.rsqrt(jnp.mean(values * values, axis=-1, keepdims=True) + EPSILON)


def rotary_apply(values, token_positions):
    half_size = values.shape[-1] // 2
    frequency = jnp.exp(
        -jnp.log(10000.0) * jnp.arange(half_size, dtype=jnp.float32) * 2.0 / values.shape[-1]
    )
    angles = token_positions[:, None] * frequency[None, :]
    cosine = jnp.cos(angles)[:, None, :]
    sine_part = jnp.sin(angles)[:, None, :]
    first_half = values[..., :half_size]
    second = values[..., half_size:]
    return jnp.concatenate(
        [first_half * cosine - second * sine_part, second * cosine + first_half * sine_part],
        axis=-1,
    )


def body(
    hidden_in,
    w_query,
    key_weight,
    value_weight,
    w_out,
    cached_prefix_keys,
    cached_prefix_values,
    doc_ids,
    routes,
    gate_scores,
    expert_in,
    expert_out,
):
    rows_dev = hidden_in.shape[0]
    column_list = hidden_in.shape[1]
    head_size = HEAD_WIDTH
    kv_local = key_weight.shape[1] // head_size
    group_width = w_query.shape[1] // head_size // kv_local
    seq_count = lax.axis_size(SEQ)
    prefix_len = cached_prefix_keys.shape[0] * seq_count
    doc_row = doc_ids[0]
    row_index = jnp.arange(rows_dev, dtype=jnp.int32)
    same_doc = doc_row[:, None] == doc_row[None, :]
    doc_start = jnp.min(jnp.where(same_doc, row_index[None, :], rows_dev), axis=1)
    token_positions = (prefix_len + row_index - doc_start).astype(jnp.float32)
    normed_input = normalize(hidden_in).astype(jnp.bfloat16)
    query_rows_all = jnp.dot(normed_input, w_query, preferred_element_type=jnp.float32).reshape(
        rows_dev, kv_local * group_width, head_size
    )
    query_rows_all = (
        rotary_apply(query_rows_all, token_positions)
        .astype(jnp.bfloat16)
        .reshape(rows_dev, kv_local, group_width, head_size)
    )
    fresh_key = jnp.dot(normed_input, key_weight, preferred_element_type=jnp.float32).reshape(
        rows_dev, kv_local, head_size
    )
    fresh_key = rotary_apply(fresh_key, token_positions).astype(jnp.bfloat16)
    fresh_value = (
        jnp.dot(normed_input, value_weight, preferred_element_type=jnp.float32)
        .astype(jnp.bfloat16)
        .reshape(rows_dev, kv_local, head_size)
    )
    own_scores = (
        jnp.einsum("tkgd,skd->tkgs", query_rows_all, fresh_key, preferred_element_type=jnp.float32)
        / head_size
    )
    visible = same_doc & (row_index[None, :] <= row_index[:, None])
    own_scores = jnp.where(visible[:, None, None, :], own_scores, -jnp.inf)
    row_top = jnp.max(own_scores, axis=-1)
    weights = jnp.exp(own_scores - row_top[..., None])
    denominator = jnp.sum(weights, axis=-1)
    numerator = jnp.einsum(
        "tkgs,skd->tkgd",
        weights.astype(jnp.bfloat16),
        fresh_value,
        preferred_element_type=jnp.float32,
    )
    running = (row_top, denominator, numerator)
    prefix_both = jnp.concatenate([cached_prefix_keys, cached_prefix_values], axis=1)
    whole_both = lax.all_gather(prefix_both, SEQ, axis=0, tiled=True)
    kv_cols = cached_prefix_keys.shape[1]
    whole_keys = whole_both[:, :kv_cols]
    whole_values = whole_both[:, kv_cols:]
    top_old, denom_old, numer_old = running
    key_rows = whole_keys.reshape(-1, kv_local, head_size)
    value_rows = whole_values.reshape(-1, kv_local, head_size)
    scores = (
        jnp.einsum("tkgd,pkd->tkgp", query_rows_all, key_rows, preferred_element_type=jnp.float32)
        / head_size
    )
    top_new = jnp.maximum(top_old, jnp.max(scores, axis=-1))
    shrink = jnp.exp(top_old - top_new)
    part_weights = jnp.exp(scores - top_new[..., None])
    denom_new = denom_old * shrink + jnp.sum(part_weights, axis=-1)
    numer_new = numer_old * shrink[..., None] + jnp.einsum(
        "tkgp,pkd->tkgd",
        part_weights.astype(jnp.bfloat16),
        value_rows,
        preferred_element_type=jnp.float32,
    )
    running = (top_new, denom_new, numer_new)
    attended = (
        (running[2] / running[1][..., None])
        .astype(jnp.bfloat16)
        .reshape(rows_dev, kv_local * group_width * head_size)
    )
    moe_rows = routes.shape[0]
    row_start = lax.axis_index("tp") * moe_rows
    attn_sum = lax.psum_scatter(
        jnp.dot(attended, w_out, preferred_element_type=jnp.float32), "tp", scatter_dimension=0, tiled=True
    )
    residual = (
        lax.dynamic_slice_in_dim(hidden_in, row_start, moe_rows, 0).astype(jnp.float32)
        + RESIDUAL * attn_sum
    )
    routed = normalize(residual).astype(jnp.bfloat16)
    experts = EXPERTS
    capacity = moe_rows // 2
    ff_part = expert_out.shape[1]
    onehot = (routes[:, :, None] == jnp.arange(experts, dtype=jnp.int32)[None, None, :]).astype(
        jnp.int32
    )
    per_row = jnp.sum(onehot, axis=1)
    before = jnp.cumsum(per_row, axis=0) - per_row
    rank_in = jnp.sum(onehot * before[:, None, :], axis=2)
    slot_of = routes * capacity + rank_in
    slot_ids = jnp.arange(experts * capacity, dtype=jnp.int32)
    pick_hit = slot_of[:, :, None] == slot_ids[None, None, :]
    selector = jnp.any(pick_hit, axis=1).T.astype(jnp.bfloat16)
    combiner = jnp.sum(jnp.where(pick_hit, gate_scores[:, :, None], 0.0), axis=1)
    gathered = jnp.dot(selector, routed, preferred_element_type=jnp.float32).astype(jnp.bfloat16)
    outgoing = gathered.reshape(experts, capacity, column_list)
    incoming = lax.all_to_all(outgoing, EXPERT_AXES, split_axis=0, concat_axis=0, tiled=True)
    incoming = incoming.reshape(experts * capacity, column_list)
    full_in = lax.all_gather(expert_in, PART_AXES, axis=0, tiled=True)
    full_out = lax.all_gather(expert_out, PART_AXES, axis=0, tiled=True)
    gate_up = jnp.einsum("rd,pdf->prf", incoming, full_in, preferred_element_type=jnp.float32)
    activated = (jax.nn.silu(gate_up[..., :ff_part]) * gate_up[..., ff_part:]).astype(jnp.bfloat16)
    partial_value = jnp.einsum(
        "prf,pfd->prd", activated, full_out, preferred_element_type=jnp.float32
    ).astype(jnp.bfloat16)
    part_total = jnp.sum(partial_value.astype(jnp.float32), axis=0).astype(jnp.bfloat16)
    returned = lax.all_to_all(
        part_total.reshape(experts, capacity, column_list), EXPERT_AXES, split_axis=0, concat_axis=0, tiled=True
    )
    part_sum = returned.reshape(experts * capacity, column_list).astype(jnp.float32)
    expert_sum = jnp.dot(
        combiner, part_sum, precision=lax.Precision.HIGHEST, preferred_element_type=jnp.float32
    )
    layer_out = (residual + RESIDUAL * expert_sum).astype(jnp.bfloat16)
    return (attn_sum.astype(jnp.bfloat16), expert_sum.astype(jnp.bfloat16), layer_out)


def solution(mesh):
    seq_size = mesh.shape["seq"]
    tp_size = mesh.shape["tp"]
    split = (seq_size // 16, 4, 2, 2, tp_size)
    fine_mesh = Mesh(mesh.devices.reshape(split), ("z", "yh", "yl", "c", "tp"))
    seq_spec = SEQ
    in_specs = (
        P(seq_spec, None),
        P(None, "tp"),
        P(None, "tp"),
        P(None, "tp"),
        P("tp", None),
        P(seq_spec, "tp"),
        P(seq_spec, "tp"),
        P(seq_spec, None),
        P(SEQ + ("tp",), None),
        P(SEQ + ("tp",), None),
        P(seq_spec, None, None),
        P(seq_spec, None, None),
    )
    out_specs = (P(SEQ + ("tp",), None),) * 3
    return jax.shard_map(body, mesh=fine_mesh, in_specs=in_specs, out_specs=out_specs, check_vma=False)
```

```python
import jax
import jax.numpy as jnp
from jax import lax
from jax.sharding import Mesh, PartitionSpec as P

HEAD_WIDTH = 64
EXPERTS = 32


SEQ = ("z", "yh", "yl", "c")
EXPERT_AXES = ("z", "yh")
PART_AXES = ("yl", "c")

EPSILON = 1e-06
RESIDUAL = 0.22


def normalize(values):
    values = values.astype(jnp.float32)
    return values * lax.rsqrt(jnp.mean(values * values, axis=-1, keepdims=True) + EPSILON)


def rotary_apply(values, token_positions):
    half_size = values.shape[-1] // 2
    frequency = jnp.exp(
        -jnp.log(10000.0) * jnp.arange(half_size, dtype=jnp.float32) * 2.0 / values.shape[-1]
    )
    angles = token_positions[:, None] * frequency[None, :]
    cosine = jnp.cos(angles)[:, None, :]
    sine_part = jnp.sin(angles)[:, None, :]
    first_half = values[..., :half_size]
    second = values[..., half_size:]
    return jnp.concatenate(
        [first_half * cosine - second * sine_part, second * cosine + first_half * sine_part],
        axis=-1,
    )


def group_gather(local):
    count = lax.axis_size(PART_AXES)
    pieces = [local]
    for shift in range(1, count):
        ring = [(i, (i + shift) % count) for i in range(count)]
        pieces.append(lax.ppermute(local, PART_AXES, ring))
    return jnp.concatenate(pieces, axis=0)


def body(
    hidden_in,
    w_query,
    key_weight,
    value_weight,
    w_out,
    cached_prefix_keys,
    cached_prefix_values,
    doc_ids,
    routes,
    gate_scores,
    expert_in,
    expert_out,
):
    rows_dev = hidden_in.shape[0]
    column_list = hidden_in.shape[1]
    head_size = HEAD_WIDTH
    kv_local = key_weight.shape[1] // head_size
    group_width = w_query.shape[1] // head_size // kv_local
    seq_count = lax.axis_size(SEQ)
    prefix_len = cached_prefix_keys.shape[0] * seq_count
    doc_row = doc_ids[0]
    row_index = jnp.arange(rows_dev, dtype=jnp.int32)
    same_doc = doc_row[:, None] == doc_row[None, :]
    doc_start = jnp.min(jnp.where(same_doc, row_index[None, :], rows_dev), axis=1)
    token_positions = (prefix_len + row_index - doc_start).astype(jnp.float32)
    normed_input = normalize(hidden_in).astype(jnp.bfloat16)
    query_rows_all = jnp.dot(normed_input, w_query, preferred_element_type=jnp.float32).reshape(
        rows_dev, kv_local * group_width, head_size
    )
    query_rows_all = (
        rotary_apply(query_rows_all, token_positions)
        .astype(jnp.bfloat16)
        .reshape(rows_dev, kv_local, group_width, head_size)
    )
    fresh_key = jnp.dot(normed_input, key_weight, preferred_element_type=jnp.float32).reshape(
        rows_dev, kv_local, head_size
    )
    fresh_key = rotary_apply(fresh_key, token_positions).astype(jnp.bfloat16)
    fresh_value = (
        jnp.dot(normed_input, value_weight, preferred_element_type=jnp.float32)
        .astype(jnp.bfloat16)
        .reshape(rows_dev, kv_local, head_size)
    )
    own_scores = (
        jnp.einsum("tkgd,skd->tkgs", query_rows_all, fresh_key, preferred_element_type=jnp.float32)
        / head_size
    )
    visible = same_doc & (row_index[None, :] <= row_index[:, None])
    own_scores = jnp.where(visible[:, None, None, :], own_scores, -jnp.inf)
    row_top = jnp.max(own_scores, axis=-1)
    weights = jnp.exp(own_scores - row_top[..., None])
    denominator = jnp.sum(weights, axis=-1)
    numerator = jnp.einsum(
        "tkgs,skd->tkgd",
        weights.astype(jnp.bfloat16),
        fresh_value,
        preferred_element_type=jnp.float32,
    )
    running = (row_top, denominator, numerator)
    prefix_both = jnp.concatenate([cached_prefix_keys, cached_prefix_values], axis=1)
    seq_total = prefix_len // prefix_both.shape[0]
    whole_both = lax.all_to_all(
        jnp.broadcast_to(prefix_both[None], (seq_total,) + prefix_both.shape), SEQ, 0, 0, tiled=True
    ).reshape(prefix_len, prefix_both.shape[1])
    kv_cols = cached_prefix_keys.shape[1]
    whole_keys = whole_both[:, :kv_cols]
    whole_values = whole_both[:, kv_cols:]
    top_old, denom_old, numer_old = running
    key_rows = whole_keys.reshape(-1, kv_local, head_size)
    value_rows = whole_values.reshape(-1, kv_local, head_size)
    scores = (
        jnp.einsum("tkgd,pkd->tkgp", query_rows_all, key_rows, preferred_element_type=jnp.float32)
        / head_size
    )
    top_new = jnp.maximum(top_old, jnp.max(scores, axis=-1))
    shrink = jnp.exp(top_old - top_new)
    part_weights = jnp.exp(scores - top_new[..., None])
    denom_new = denom_old * shrink + jnp.sum(part_weights, axis=-1)
    numer_new = numer_old * shrink[..., None] + jnp.einsum(
        "tkgp,pkd->tkgd",
        part_weights.astype(jnp.bfloat16),
        value_rows,
        preferred_element_type=jnp.float32,
    )
    running = (top_new, denom_new, numer_new)
    attended = (
        (running[2] / running[1][..., None])
        .astype(jnp.bfloat16)
        .reshape(rows_dev, kv_local * group_width * head_size)
    )
    moe_rows = routes.shape[0]
    row_start = lax.axis_index("tp") * moe_rows
    attn_part = jnp.dot(attended, w_out, preferred_element_type=jnp.float32)
    tp_index = lax.axis_index("tp")
    tp_count = lax.axis_size("tp")
    attn_sum = lax.dynamic_slice_in_dim(attn_part, row_start, moe_rows, 0)
    for shift in range(1, tp_count):
        target = (tp_index + shift) % tp_count
        sent = lax.dynamic_slice_in_dim(attn_part, target * moe_rows, moe_rows, 0)
        ring = [(i, (i + shift) % tp_count) for i in range(tp_count)]
        attn_sum = attn_sum + lax.ppermute(sent, "tp", ring)
    residual = (
        lax.dynamic_slice_in_dim(hidden_in, row_start, moe_rows, 0).astype(jnp.float32)
        + RESIDUAL * attn_sum
    )
    routed = normalize(residual).astype(jnp.bfloat16)
    experts = EXPERTS
    capacity = moe_rows // 2
    ff_part = expert_out.shape[1]
    onehot = (routes[:, :, None] == jnp.arange(experts, dtype=jnp.int32)[None, None, :]).astype(
        jnp.int32
    )
    per_row = jnp.sum(onehot, axis=1)
    before = jnp.cumsum(per_row, axis=0) - per_row
    rank_in = jnp.sum(onehot * before[:, None, :], axis=2)
    slot_of = routes * capacity + rank_in
    slot_ids = jnp.arange(experts * capacity, dtype=jnp.int32)
    pick_hit = slot_of[:, :, None] == slot_ids[None, None, :]
    selector = jnp.any(pick_hit, axis=1).T.astype(jnp.bfloat16)
    combiner = jnp.sum(jnp.where(pick_hit, gate_scores[:, :, None], 0.0), axis=1)
    gathered = jnp.dot(selector, routed, preferred_element_type=jnp.float32).astype(jnp.bfloat16)
    outgoing = gathered.reshape(experts, capacity, column_list)
    incoming = lax.all_to_all(outgoing, EXPERT_AXES, split_axis=0, concat_axis=0, tiled=True)
    incoming = incoming.reshape(experts * capacity, column_list)
    full_in = group_gather(expert_in)
    full_out = group_gather(expert_out)
    gate_up = jnp.einsum("rd,pdf->prf", incoming, full_in, preferred_element_type=jnp.float32)
    activated = (jax.nn.silu(gate_up[..., :ff_part]) * gate_up[..., ff_part:]).astype(jnp.bfloat16)
    partial_value = jnp.einsum(
        "prf,pfd->prd", activated, full_out, preferred_element_type=jnp.float32
    ).astype(jnp.bfloat16)
    part_total = jnp.sum(partial_value.astype(jnp.float32), axis=0).astype(jnp.bfloat16)
    returned = lax.all_to_all(
        part_total.reshape(experts, capacity, column_list), EXPERT_AXES, split_axis=0, concat_axis=0, tiled=True
    )
    part_sum = returned.reshape(experts * capacity, column_list).astype(jnp.float32)
    expert_sum = jnp.dot(
        combiner, part_sum, precision=lax.Precision.HIGHEST, preferred_element_type=jnp.float32
    )
    layer_out = (residual + RESIDUAL * expert_sum).astype(jnp.bfloat16)
    return (attn_sum.astype(jnp.bfloat16), expert_sum.astype(jnp.bfloat16), layer_out)


def solution(mesh):
    seq_size = mesh.shape["seq"]
    tp_size = mesh.shape["tp"]
    split = (seq_size // 16, 4, 2, 2, tp_size)
    fine_mesh = Mesh(mesh.devices.reshape(split), ("z", "yh", "yl", "c", "tp"))
    seq_spec = SEQ
    in_specs = (
        P(seq_spec, None),
        P(None, "tp"),
        P(None, "tp"),
        P(None, "tp"),
        P("tp", None),
        P(seq_spec, "tp"),
        P(seq_spec, "tp"),
        P(seq_spec, None),
        P(SEQ + ("tp",), None),
        P(SEQ + ("tp",), None),
        P(seq_spec, None, None),
        P(seq_spec, None, None),
    )
    out_specs = (P(SEQ + ("tp",), None),) * 3
    return jax.shard_map(body, mesh=fine_mesh, in_specs=in_specs, out_specs=out_specs, check_vma=False)
```

```python
import jax
import jax.numpy as jnp
from jax import lax
from jax.sharding import Mesh, PartitionSpec as P

HEAD_WIDTH = 64
EXPERTS = 32


SEQ = ("z", "yh", "yl", "c")
EXPERT_AXES = ("z", "yh")
PART_AXES = ("yl", "c")

EPSILON = 1e-06
RESIDUAL = 0.22


def normalize(values):
    values = values.astype(jnp.float32)
    return values * lax.rsqrt(jnp.mean(values * values, axis=-1, keepdims=True) + EPSILON)


def rotary_apply(values, token_positions):
    half_size = values.shape[-1] // 2
    frequency = jnp.exp(
        -jnp.log(10000.0) * jnp.arange(half_size, dtype=jnp.float32) * 2.0 / values.shape[-1]
    )
    angles = token_positions[:, None] * frequency[None, :]
    cosine = jnp.cos(angles)[:, None, :]
    sine_part = jnp.sin(angles)[:, None, :]
    first_half = values[..., :half_size]
    second = values[..., half_size:]
    return jnp.concatenate(
        [first_half * cosine - second * sine_part, second * cosine + first_half * sine_part],
        axis=-1,
    )


def body(
    hidden_in,
    w_query,
    key_weight,
    value_weight,
    w_out,
    cached_prefix_keys,
    cached_prefix_values,
    doc_ids,
    routes,
    gate_scores,
    expert_in,
    expert_out,
):
    in_cols = expert_in.shape[2]
    packed = jnp.concatenate(
        [expert_in, expert_out.reshape(expert_out.shape[0], expert_in.shape[1], -1)], axis=2
    )
    packed = lax.all_gather(packed, PART_AXES, axis=0, tiled=True)
    full_in = packed[..., :in_cols]
    full_out = packed[..., in_cols:].reshape((packed.shape[0],) + expert_out.shape[1:])
    rows_dev = hidden_in.shape[0]
    column_list = hidden_in.shape[1]
    head_size = HEAD_WIDTH
    kv_local = key_weight.shape[1] // head_size
    group_width = w_query.shape[1] // head_size // kv_local
    seq_count = lax.axis_size(SEQ)
    prefix_len = cached_prefix_keys.shape[0] * seq_count
    doc_row = doc_ids[0]
    row_index = jnp.arange(rows_dev, dtype=jnp.int32)
    same_doc = doc_row[:, None] == doc_row[None, :]
    doc_start = jnp.min(jnp.where(same_doc, row_index[None, :], rows_dev), axis=1)
    token_positions = (prefix_len + row_index - doc_start).astype(jnp.float32)
    normed_input = normalize(hidden_in).astype(jnp.bfloat16)
    query_rows_all = jnp.dot(normed_input, w_query, preferred_element_type=jnp.float32).reshape(
        rows_dev, kv_local * group_width, head_size
    )
    query_rows_all = (
        rotary_apply(query_rows_all, token_positions)
        .astype(jnp.bfloat16)
        .reshape(rows_dev, kv_local, group_width, head_size)
    )
    fresh_key = jnp.dot(normed_input, key_weight, preferred_element_type=jnp.float32).reshape(
        rows_dev, kv_local, head_size
    )
    fresh_key = rotary_apply(fresh_key, token_positions).astype(jnp.bfloat16)
    fresh_value = (
        jnp.dot(normed_input, value_weight, preferred_element_type=jnp.float32)
        .astype(jnp.bfloat16)
        .reshape(rows_dev, kv_local, head_size)
    )
    own_scores = (
        jnp.einsum("tkgd,skd->tkgs", query_rows_all, fresh_key, preferred_element_type=jnp.float32)
        / head_size
    )
    visible = same_doc & (row_index[None, :] <= row_index[:, None])
    own_scores = jnp.where(visible[:, None, None, :], own_scores, -jnp.inf)
    row_top = jnp.max(own_scores, axis=-1)
    weights = jnp.exp(own_scores - row_top[..., None])
    denominator = jnp.sum(weights, axis=-1)
    numerator = jnp.einsum(
        "tkgs,skd->tkgd",
        weights.astype(jnp.bfloat16),
        fresh_value,
        preferred_element_type=jnp.float32,
    )
    running = (row_top, denominator, numerator)
    prefix_both = jnp.concatenate([cached_prefix_keys, cached_prefix_values], axis=1)
    seq_total = prefix_len // prefix_both.shape[0]
    whole_both = lax.all_to_all(
        jnp.broadcast_to(prefix_both[None], (seq_total,) + prefix_both.shape), SEQ, 0, 0, tiled=True
    ).reshape(prefix_len, prefix_both.shape[1])
    kv_cols = cached_prefix_keys.shape[1]
    whole_keys = whole_both[:, :kv_cols]
    whole_values = whole_both[:, kv_cols:]
    top_old, denom_old, numer_old = running
    key_rows = whole_keys.reshape(-1, kv_local, head_size)
    value_rows = whole_values.reshape(-1, kv_local, head_size)
    scores = (
        jnp.einsum("tkgd,pkd->tkgp", query_rows_all, key_rows, preferred_element_type=jnp.float32)
        / head_size
    )
    top_new = jnp.maximum(top_old, jnp.max(scores, axis=-1))
    shrink = jnp.exp(top_old - top_new)
    part_weights = jnp.exp(scores - top_new[..., None])
    denom_new = denom_old * shrink + jnp.sum(part_weights, axis=-1)
    numer_new = numer_old * shrink[..., None] + jnp.einsum(
        "tkgp,pkd->tkgd",
        part_weights.astype(jnp.bfloat16),
        value_rows,
        preferred_element_type=jnp.float32,
    )
    running = (top_new, denom_new, numer_new)
    attended = (
        (running[2] / running[1][..., None])
        .astype(jnp.bfloat16)
        .reshape(rows_dev, kv_local * group_width * head_size)
    )
    moe_rows = routes.shape[0]
    row_start = lax.axis_index("tp") * moe_rows
    attn_part = jnp.dot(attended, w_out, preferred_element_type=jnp.float32)
    tp_index = lax.axis_index("tp")
    tp_count = lax.axis_size("tp")
    attn_sum = lax.dynamic_slice_in_dim(attn_part, row_start, moe_rows, 0)
    for shift in range(1, tp_count):
        target = (tp_index + shift) % tp_count
        sent = lax.dynamic_slice_in_dim(attn_part, target * moe_rows, moe_rows, 0)
        ring = [(i, (i + shift) % tp_count) for i in range(tp_count)]
        attn_sum = attn_sum + lax.ppermute(sent, "tp", ring)
    residual = (
        lax.dynamic_slice_in_dim(hidden_in, row_start, moe_rows, 0).astype(jnp.float32)
        + RESIDUAL * attn_sum
    )
    routed = normalize(residual).astype(jnp.bfloat16)
    experts = EXPERTS
    capacity = moe_rows // 2
    ff_part = expert_out.shape[1]
    onehot = (routes[:, :, None] == jnp.arange(experts, dtype=jnp.int32)[None, None, :]).astype(
        jnp.int32
    )
    per_row = jnp.sum(onehot, axis=1)
    before = jnp.cumsum(per_row, axis=0) - per_row
    rank_in = jnp.sum(onehot * before[:, None, :], axis=2)
    slot_of = routes * capacity + rank_in
    slot_ids = jnp.arange(experts * capacity, dtype=jnp.int32)
    pick_hit = slot_of[:, :, None] == slot_ids[None, None, :]
    selector = jnp.any(pick_hit, axis=1).T.astype(jnp.bfloat16)
    combiner = jnp.sum(jnp.where(pick_hit, gate_scores[:, :, None], 0.0), axis=1)
    gathered = jnp.dot(selector, routed, preferred_element_type=jnp.float32).astype(jnp.bfloat16)
    outgoing = gathered.reshape(experts, capacity, column_list)
    incoming = lax.all_to_all(outgoing, EXPERT_AXES, split_axis=0, concat_axis=0, tiled=True)
    incoming = incoming.reshape(experts * capacity, column_list)
    gate_up = jnp.einsum("rd,pdf->prf", incoming, full_in, preferred_element_type=jnp.float32)
    activated = (jax.nn.silu(gate_up[..., :ff_part]) * gate_up[..., ff_part:]).astype(jnp.bfloat16)
    partial_value = jnp.einsum(
        "prf,pfd->prd", activated, full_out, preferred_element_type=jnp.float32
    ).astype(jnp.bfloat16)
    part_total = jnp.sum(partial_value.astype(jnp.float32), axis=0).astype(jnp.bfloat16)
    returned = lax.all_to_all(
        part_total.reshape(experts, capacity, column_list), EXPERT_AXES, split_axis=0, concat_axis=0, tiled=True
    )
    part_sum = returned.reshape(experts * capacity, column_list).astype(jnp.float32)
    expert_sum = jnp.dot(
        combiner, part_sum, precision=lax.Precision.HIGHEST, preferred_element_type=jnp.float32
    )
    layer_out = (residual + RESIDUAL * expert_sum).astype(jnp.bfloat16)
    return (attn_sum.astype(jnp.bfloat16), expert_sum.astype(jnp.bfloat16), layer_out)


def solution(mesh):
    seq_size = mesh.shape["seq"]
    tp_size = mesh.shape["tp"]
    split = (seq_size // 16, 4, 2, 2, tp_size)
    fine_mesh = Mesh(mesh.devices.reshape(split), ("z", "yh", "yl", "c", "tp"))
    seq_spec = SEQ
    in_specs = (
        P(seq_spec, None),
        P(None, "tp"),
        P(None, "tp"),
        P(None, "tp"),
        P("tp", None),
        P(seq_spec, "tp"),
        P(seq_spec, "tp"),
        P(seq_spec, None),
        P(SEQ + ("tp",), None),
        P(SEQ + ("tp",), None),
        P(seq_spec, None, None),
        P(seq_spec, None, None),
    )
    out_specs = (P(SEQ + ("tp",), None),) * 3
    return jax.shard_map(body, mesh=fine_mesh, in_specs=in_specs, out_specs=out_specs, check_vma=False)
```

```python
import jax
import jax.numpy as jnp
from jax import lax
from jax.sharding import Mesh, PartitionSpec as P

HEAD_WIDTH = 64
EXPERTS = 32


SEQ = ("z", "yh", "yl", "c")
EXPERT_AXES = ("z", "yh")
PART_AXES = ("yl", "c")

EPSILON = 1e-06
RESIDUAL = 0.22


def normalize(values):
    values = values.astype(jnp.float32)
    return values * lax.rsqrt(jnp.mean(values * values, axis=-1, keepdims=True) + EPSILON)


def rotary_apply(values, token_positions):
    half_size = values.shape[-1] // 2
    frequency = jnp.exp(
        -jnp.log(10000.0) * jnp.arange(half_size, dtype=jnp.float32) * 2.0 / values.shape[-1]
    )
    angles = token_positions[:, None] * frequency[None, :]
    cosine = jnp.cos(angles)[:, None, :]
    sine_part = jnp.sin(angles)[:, None, :]
    first_half = values[..., :half_size]
    second = values[..., half_size:]
    return jnp.concatenate(
        [first_half * cosine - second * sine_part, second * cosine + first_half * sine_part],
        axis=-1,
    )


def group_gather(local):
    count = lax.axis_size(PART_AXES)
    pieces = [local]
    for shift in range(1, count):
        ring = [(i, (i + shift) % count) for i in range(count)]
        pieces.append(lax.ppermute(local, PART_AXES, ring))
    return jnp.concatenate(pieces, axis=0)


def body(
    hidden_in,
    w_query,
    key_weight,
    value_weight,
    w_out,
    cached_prefix_keys,
    cached_prefix_values,
    doc_ids,
    routes,
    gate_scores,
    expert_in,
    expert_out,
):
    rows_dev = hidden_in.shape[0]
    column_list = hidden_in.shape[1]
    head_size = HEAD_WIDTH
    kv_local = key_weight.shape[1] // head_size
    group_width = w_query.shape[1] // head_size // kv_local
    seq_count = lax.axis_size(SEQ)
    prefix_len = cached_prefix_keys.shape[0] * seq_count
    doc_row = doc_ids[0]
    row_index = jnp.arange(rows_dev, dtype=jnp.int32)
    same_doc = doc_row[:, None] == doc_row[None, :]
    doc_start = jnp.min(jnp.where(same_doc, row_index[None, :], rows_dev), axis=1)
    token_positions = (prefix_len + row_index - doc_start).astype(jnp.float32)
    normed_input = normalize(hidden_in).astype(jnp.bfloat16)
    query_rows_all = jnp.dot(normed_input, w_query, preferred_element_type=jnp.float32).reshape(
        rows_dev, kv_local * group_width, head_size
    )
    query_rows_all = (
        rotary_apply(query_rows_all, token_positions)
        .astype(jnp.bfloat16)
        .reshape(rows_dev, kv_local, group_width, head_size)
    )
    fresh_key = jnp.dot(normed_input, key_weight, preferred_element_type=jnp.float32).reshape(
        rows_dev, kv_local, head_size
    )
    fresh_key = rotary_apply(fresh_key, token_positions).astype(jnp.bfloat16)
    fresh_value = (
        jnp.dot(normed_input, value_weight, preferred_element_type=jnp.float32)
        .astype(jnp.bfloat16)
        .reshape(rows_dev, kv_local, head_size)
    )
    own_scores = (
        jnp.einsum("tkgd,skd->tkgs", query_rows_all, fresh_key, preferred_element_type=jnp.float32)
        / head_size
    )
    visible = same_doc & (row_index[None, :] <= row_index[:, None])
    own_scores = jnp.where(visible[:, None, None, :], own_scores, -jnp.inf)
    row_top = jnp.max(own_scores, axis=-1)
    weights = jnp.exp(own_scores - row_top[..., None])
    denominator = jnp.sum(weights, axis=-1)
    numerator = jnp.einsum(
        "tkgs,skd->tkgd",
        weights.astype(jnp.bfloat16),
        fresh_value,
        preferred_element_type=jnp.float32,
    )
    running = (row_top, denominator, numerator)
    prefix_both = jnp.concatenate([cached_prefix_keys, cached_prefix_values], axis=1)
    seq_total = prefix_len // prefix_both.shape[0]
    whole_both = lax.all_to_all(
        jnp.broadcast_to(prefix_both[None], (seq_total,) + prefix_both.shape), SEQ, 0, 0, tiled=True
    ).reshape(prefix_len, prefix_both.shape[1])
    full_in = group_gather(expert_in)
    full_out = group_gather(expert_out)
    whole_both, full_in, full_out = lax.optimization_barrier((whole_both, full_in, full_out))
    kv_cols = cached_prefix_keys.shape[1]
    whole_keys = whole_both[:, :kv_cols]
    whole_values = whole_both[:, kv_cols:]
    top_old, denom_old, numer_old = running
    key_rows = whole_keys.reshape(-1, kv_local, head_size)
    value_rows = whole_values.reshape(-1, kv_local, head_size)
    scores = (
        jnp.einsum("tkgd,pkd->tkgp", query_rows_all, key_rows, preferred_element_type=jnp.float32)
        / head_size
    )
    top_new = jnp.maximum(top_old, jnp.max(scores, axis=-1))
    shrink = jnp.exp(top_old - top_new)
    part_weights = jnp.exp(scores - top_new[..., None])
    denom_new = denom_old * shrink + jnp.sum(part_weights, axis=-1)
    numer_new = numer_old * shrink[..., None] + jnp.einsum(
        "tkgp,pkd->tkgd",
        part_weights.astype(jnp.bfloat16),
        value_rows,
        preferred_element_type=jnp.float32,
    )
    running = (top_new, denom_new, numer_new)
    attended = (
        (running[2] / running[1][..., None])
        .astype(jnp.bfloat16)
        .reshape(rows_dev, kv_local * group_width * head_size)
    )
    moe_rows = routes.shape[0]
    row_start = lax.axis_index("tp") * moe_rows
    attn_part = jnp.dot(attended, w_out, preferred_element_type=jnp.float32)
    tp_index = lax.axis_index("tp")
    tp_count = lax.axis_size("tp")
    attn_sum = lax.dynamic_slice_in_dim(attn_part, row_start, moe_rows, 0)
    for shift in range(1, tp_count):
        target = (tp_index + shift) % tp_count
        sent = lax.dynamic_slice_in_dim(attn_part, target * moe_rows, moe_rows, 0)
        ring = [(i, (i + shift) % tp_count) for i in range(tp_count)]
        attn_sum = attn_sum + lax.ppermute(sent, "tp", ring)
    residual = (
        lax.dynamic_slice_in_dim(hidden_in, row_start, moe_rows, 0).astype(jnp.float32)
        + RESIDUAL * attn_sum
    )
    routed = normalize(residual).astype(jnp.bfloat16)
    experts = EXPERTS
    capacity = moe_rows // 2
    ff_part = expert_out.shape[1]
    onehot = (routes[:, :, None] == jnp.arange(experts, dtype=jnp.int32)[None, None, :]).astype(
        jnp.int32
    )
    per_row = jnp.sum(onehot, axis=1)
    before = jnp.cumsum(per_row, axis=0) - per_row
    rank_in = jnp.sum(onehot * before[:, None, :], axis=2)
    slot_of = routes * capacity + rank_in
    slot_ids = jnp.arange(experts * capacity, dtype=jnp.int32)
    pick_hit = slot_of[:, :, None] == slot_ids[None, None, :]
    selector = jnp.any(pick_hit, axis=1).T.astype(jnp.bfloat16)
    combiner = jnp.sum(jnp.where(pick_hit, gate_scores[:, :, None], 0.0), axis=1)
    gathered = jnp.dot(selector, routed, preferred_element_type=jnp.float32).astype(jnp.bfloat16)
    outgoing = gathered.reshape(experts, capacity, column_list)
    incoming = lax.all_to_all(outgoing, EXPERT_AXES, split_axis=0, concat_axis=0, tiled=True)
    incoming = incoming.reshape(experts * capacity, column_list)
    gate_up = jnp.einsum("rd,pdf->prf", incoming, full_in, preferred_element_type=jnp.float32)
    activated = (jax.nn.silu(gate_up[..., :ff_part]) * gate_up[..., ff_part:]).astype(jnp.bfloat16)
    partial_value = jnp.einsum(
        "prf,pfd->prd", activated, full_out, preferred_element_type=jnp.float32
    ).astype(jnp.bfloat16)
    part_total = jnp.sum(partial_value.astype(jnp.float32), axis=0).astype(jnp.bfloat16)
    returned = lax.all_to_all(
        part_total.reshape(experts, capacity, column_list), EXPERT_AXES, split_axis=0, concat_axis=0, tiled=True
    )
    part_sum = returned.reshape(experts * capacity, column_list).astype(jnp.float32)
    expert_sum = jnp.dot(
        combiner, part_sum, precision=lax.Precision.HIGHEST, preferred_element_type=jnp.float32
    )
    layer_out = (residual + RESIDUAL * expert_sum).astype(jnp.bfloat16)
    return (attn_sum.astype(jnp.bfloat16), expert_sum.astype(jnp.bfloat16), layer_out)


def solution(mesh):
    seq_size = mesh.shape["seq"]
    tp_size = mesh.shape["tp"]
    split = (seq_size // 16, 4, 2, 2, tp_size)
    fine_mesh = Mesh(mesh.devices.reshape(split), ("z", "yh", "yl", "c", "tp"))
    seq_spec = SEQ
    in_specs = (
        P(seq_spec, None),
        P(None, "tp"),
        P(None, "tp"),
        P(None, "tp"),
        P("tp", None),
        P(seq_spec, "tp"),
        P(seq_spec, "tp"),
        P(seq_spec, None),
        P(SEQ + ("tp",), None),
        P(SEQ + ("tp",), None),
        P(seq_spec, None, None),
        P(seq_spec, None, None),
    )
    out_specs = (P(SEQ + ("tp",), None),) * 3
    return jax.shard_map(body, mesh=fine_mesh, in_specs=in_specs, out_specs=out_specs, check_vma=False)
```

```python
import jax
import jax.numpy as jnp
from jax import lax
from jax.sharding import Mesh, PartitionSpec as P

HEAD_WIDTH = 64
EXPERTS = 32


SEQ = ("z", "yh", "yl", "c")
EXPERT_AXES = ("z", "yh")
PART_AXES = ("yl", "c")

EPSILON = 1e-06
RESIDUAL = 0.22


def normalize(values):
    values = values.astype(jnp.float32)
    return values * lax.rsqrt(jnp.mean(values * values, axis=-1, keepdims=True) + EPSILON)


def rotary_apply(values, token_positions):
    half_size = values.shape[-1] // 2
    frequency = jnp.exp(
        -jnp.log(10000.0) * jnp.arange(half_size, dtype=jnp.float32) * 2.0 / values.shape[-1]
    )
    angles = token_positions[:, None] * frequency[None, :]
    cosine = jnp.cos(angles)[:, None, :]
    sine_part = jnp.sin(angles)[:, None, :]
    first_half = values[..., :half_size]
    second = values[..., half_size:]
    return jnp.concatenate(
        [first_half * cosine - second * sine_part, second * cosine + first_half * sine_part],
        axis=-1,
    )


def body(
    hidden_in,
    w_query,
    key_weight,
    value_weight,
    w_out,
    cached_prefix_keys,
    cached_prefix_values,
    doc_ids,
    routes,
    gate_scores,
    expert_in,
    expert_out,
):
    in_cols = expert_in.shape[2]
    packed = jnp.concatenate(
        [expert_in, expert_out.reshape(expert_out.shape[0], expert_in.shape[1], -1)], axis=2
    )
    packed = lax.all_gather(packed, PART_AXES, axis=0, tiled=True)
    full_in = packed[..., :in_cols]
    full_out = packed[..., in_cols:].reshape((packed.shape[0],) + expert_out.shape[1:])
    rows_dev = hidden_in.shape[0]
    column_list = hidden_in.shape[1]
    head_size = HEAD_WIDTH
    kv_local = key_weight.shape[1] // head_size
    group_width = w_query.shape[1] // head_size // kv_local
    seq_count = lax.axis_size(SEQ)
    prefix_len = cached_prefix_keys.shape[0] * seq_count
    doc_row = doc_ids[0]
    row_index = jnp.arange(rows_dev, dtype=jnp.int32)
    same_doc = doc_row[:, None] == doc_row[None, :]
    doc_start = jnp.min(jnp.where(same_doc, row_index[None, :], rows_dev), axis=1)
    token_positions = (prefix_len + row_index - doc_start).astype(jnp.float32)
    normed_input = normalize(hidden_in).astype(jnp.bfloat16)
    query_rows_all = jnp.dot(normed_input, w_query, preferred_element_type=jnp.float32).reshape(
        rows_dev, kv_local * group_width, head_size
    )
    query_rows_all = (
        rotary_apply(query_rows_all, token_positions)
        .astype(jnp.bfloat16)
        .reshape(rows_dev, kv_local, group_width, head_size)
    )
    fresh_key = jnp.dot(normed_input, key_weight, preferred_element_type=jnp.float32).reshape(
        rows_dev, kv_local, head_size
    )
    fresh_key = rotary_apply(fresh_key, token_positions).astype(jnp.bfloat16)
    fresh_value = (
        jnp.dot(normed_input, value_weight, preferred_element_type=jnp.float32)
        .astype(jnp.bfloat16)
        .reshape(rows_dev, kv_local, head_size)
    )
    own_scores = (
        jnp.einsum("tkgd,skd->tkgs", query_rows_all, fresh_key, preferred_element_type=jnp.float32)
        / head_size
    )
    visible = same_doc & (row_index[None, :] <= row_index[:, None])
    own_scores = jnp.where(visible[:, None, None, :], own_scores, -jnp.inf)
    row_top = jnp.max(own_scores, axis=-1)
    weights = jnp.exp(own_scores - row_top[..., None])
    denominator = jnp.sum(weights, axis=-1)
    numerator = jnp.einsum(
        "tkgs,skd->tkgd",
        weights.astype(jnp.bfloat16),
        fresh_value,
        preferred_element_type=jnp.float32,
    )
    running = (row_top, denominator, numerator)
    prefix_both = jnp.concatenate([cached_prefix_keys, cached_prefix_values], axis=1)
    seq_total = prefix_len // prefix_both.shape[0]
    whole_both = lax.all_to_all(
        jnp.broadcast_to(prefix_both[None], (seq_total,) + prefix_both.shape), SEQ, 0, 0, tiled=True
    ).reshape(prefix_len, prefix_both.shape[1])
    kv_cols = cached_prefix_keys.shape[1]
    whole_keys = whole_both[:, :kv_cols]
    whole_values = whole_both[:, kv_cols:]
    top_old, denom_old, numer_old = running
    key_rows = whole_keys.reshape(-1, kv_local, head_size)
    value_rows = whole_values.reshape(-1, kv_local, head_size)
    scores = (
        jnp.einsum("tkgd,pkd->tkgp", query_rows_all, key_rows, preferred_element_type=jnp.float32)
        / head_size
    )
    top_new = jnp.maximum(top_old, jnp.max(scores, axis=-1))
    shrink = jnp.exp(top_old - top_new)
    part_weights = jnp.exp(scores - top_new[..., None])
    denom_new = denom_old * shrink + jnp.sum(part_weights, axis=-1)
    numer_new = numer_old * shrink[..., None] + jnp.einsum(
        "tkgp,pkd->tkgd",
        part_weights.astype(jnp.bfloat16),
        value_rows,
        preferred_element_type=jnp.float32,
    )
    running = (top_new, denom_new, numer_new)
    attended = (
        (running[2] / running[1][..., None])
        .astype(jnp.bfloat16)
        .reshape(rows_dev, kv_local * group_width * head_size)
    )
    moe_rows = routes.shape[0]
    row_start = lax.axis_index("tp") * moe_rows
    attn_part = jnp.dot(attended, w_out, preferred_element_type=jnp.float32)
    tp_count = lax.axis_size("tp")
    exchanged = lax.all_to_all(
        attn_part.reshape(tp_count, moe_rows, column_list), "tp", 0, 0, tiled=True
    )
    attn_sum = jnp.sum(exchanged, axis=0)
    residual = (
        lax.dynamic_slice_in_dim(hidden_in, row_start, moe_rows, 0).astype(jnp.float32)
        + RESIDUAL * attn_sum
    )
    routed = normalize(residual).astype(jnp.bfloat16)
    experts = EXPERTS
    capacity = moe_rows // 2
    ff_part = expert_out.shape[1]
    onehot = (routes[:, :, None] == jnp.arange(experts, dtype=jnp.int32)[None, None, :]).astype(
        jnp.int32
    )
    per_row = jnp.sum(onehot, axis=1)
    before = jnp.cumsum(per_row, axis=0) - per_row
    rank_in = jnp.sum(onehot * before[:, None, :], axis=2)
    slot_of = routes * capacity + rank_in
    slot_ids = jnp.arange(experts * capacity, dtype=jnp.int32)
    pick_hit = slot_of[:, :, None] == slot_ids[None, None, :]
    selector = jnp.any(pick_hit, axis=1).T.astype(jnp.bfloat16)
    combiner = jnp.sum(jnp.where(pick_hit, gate_scores[:, :, None], 0.0), axis=1)
    gathered = jnp.dot(selector, routed, preferred_element_type=jnp.float32).astype(jnp.bfloat16)
    outgoing = gathered.reshape(experts, capacity, column_list)
    incoming = lax.all_to_all(outgoing, EXPERT_AXES, split_axis=0, concat_axis=0, tiled=True)
    incoming = incoming.reshape(experts * capacity, column_list)
    gate_up = jnp.einsum("rd,pdf->prf", incoming, full_in, preferred_element_type=jnp.float32)
    activated = (jax.nn.silu(gate_up[..., :ff_part]) * gate_up[..., ff_part:]).astype(jnp.bfloat16)
    partial_value = jnp.einsum(
        "prf,pfd->prd", activated, full_out, preferred_element_type=jnp.float32
    ).astype(jnp.bfloat16)
    part_total = jnp.sum(partial_value.astype(jnp.float32), axis=0).astype(jnp.bfloat16)
    returned = lax.all_to_all(
        part_total.reshape(experts, capacity, column_list), EXPERT_AXES, split_axis=0, concat_axis=0, tiled=True
    )
    part_sum = returned.reshape(experts * capacity, column_list).astype(jnp.float32)
    expert_sum = jnp.dot(
        combiner, part_sum, precision=lax.Precision.HIGHEST, preferred_element_type=jnp.float32
    )
    layer_out = (residual + RESIDUAL * expert_sum).astype(jnp.bfloat16)
    return (attn_sum.astype(jnp.bfloat16), expert_sum.astype(jnp.bfloat16), layer_out)


def solution(mesh):
    seq_size = mesh.shape["seq"]
    tp_size = mesh.shape["tp"]
    split = (seq_size // 16, 4, 2, 2, tp_size)
    fine_mesh = Mesh(mesh.devices.reshape(split), ("z", "yh", "yl", "c", "tp"))
    seq_spec = SEQ
    in_specs = (
        P(seq_spec, None),
        P(None, "tp"),
        P(None, "tp"),
        P(None, "tp"),
        P("tp", None),
        P(seq_spec, "tp"),
        P(seq_spec, "tp"),
        P(seq_spec, None),
        P(SEQ + ("tp",), None),
        P(SEQ + ("tp",), None),
        P(seq_spec, None, None),
        P(seq_spec, None, None),
    )
    out_specs = (P(SEQ + ("tp",), None),) * 3
    return jax.shard_map(body, mesh=fine_mesh, in_specs=in_specs, out_specs=out_specs, check_vma=False)
```

```python
import jax
import jax.numpy as jnp
from jax import lax
from jax.experimental import pallas as pl
from jax.sharding import Mesh, PartitionSpec as P

HEAD_WIDTH = 64
EXPERTS = 32


SEQ = ("z", "yh", "yl", "c")
EXPERT_AXES = ("z", "yh")
PART_AXES = ("yl", "c")

EPSILON = 1e-06
RESIDUAL = 0.22


def normalize(values):
    values = values.astype(jnp.float32)
    return values * lax.rsqrt(jnp.mean(values * values, axis=-1, keepdims=True) + EPSILON)


def rotary_apply(values, token_positions):
    half_size = values.shape[-1] // 2
    frequency = jnp.exp(
        -jnp.log(10000.0) * jnp.arange(half_size, dtype=jnp.float32) * 2.0 / values.shape[-1]
    )
    angles = token_positions[:, None] * frequency[None, :]
    cosine = jnp.cos(angles)[:, None, :]
    sine_part = jnp.sin(angles)[:, None, :]
    first_half = values[..., :half_size]
    second = values[..., half_size:]
    return jnp.concatenate(
        [first_half * cosine - second * sine_part, second * cosine + first_half * sine_part],
        axis=-1,
    )


def prefix_attention(queries, keys_values, top_old, denom_old, numer_old, head_size):
    kv_local = queries.shape[0]
    value_base = keys_values.shape[1] // 2

    def kernel(q_ref, kv_ref, top_ref, den_ref, num_ref, out_ref):
        for head in range(kv_local):
            keys = kv_ref[:, head * head_size : (head + 1) * head_size]
            values = kv_ref[:, value_base + head * head_size : value_base + (head + 1) * head_size]
            scores = lax.dot_general(
                q_ref[head], keys, (((1,), (1,)), ((), ())), preferred_element_type=jnp.float32
            ) * (1.0 / head_size)
            top_prev = top_ref[head]
            top_new = jnp.maximum(top_prev, jnp.max(scores, axis=1, keepdims=True))
            shrink = jnp.exp(top_prev - top_new)
            weights = jnp.exp(scores - top_new)
            denom = den_ref[head] * shrink + jnp.sum(weights, axis=1, keepdims=True)
            numer = num_ref[head] * shrink + jnp.dot(
                weights.astype(jnp.bfloat16), values, preferred_element_type=jnp.float32
            )
            out_ref[head] = (numer / denom).astype(jnp.bfloat16)

    return pl.pallas_call(
        kernel, out_shape=jax.ShapeDtypeStruct(queries.shape, jnp.bfloat16)
    )(queries, keys_values, top_old, denom_old, numer_old)


def body(
    hidden_in,
    w_query,
    key_weight,
    value_weight,
    w_out,
    cached_prefix_keys,
    cached_prefix_values,
    doc_ids,
    routes,
    gate_scores,
    expert_in,
    expert_out,
):
    in_cols = expert_in.shape[2]
    packed = jnp.concatenate(
        [expert_in, expert_out.reshape(expert_out.shape[0], expert_in.shape[1], -1)], axis=2
    )
    packed = lax.all_gather(packed, PART_AXES, axis=0, tiled=True)
    full_in = packed[..., :in_cols]
    full_out = packed[..., in_cols:].reshape((packed.shape[0],) + expert_out.shape[1:])
    rows_dev = hidden_in.shape[0]
    column_list = hidden_in.shape[1]
    head_size = HEAD_WIDTH
    kv_local = key_weight.shape[1] // head_size
    group_width = w_query.shape[1] // head_size // kv_local
    seq_count = lax.axis_size(SEQ)
    prefix_len = cached_prefix_keys.shape[0] * seq_count
    doc_row = doc_ids[0]
    row_index = jnp.arange(rows_dev, dtype=jnp.int32)
    same_doc = doc_row[:, None] == doc_row[None, :]
    doc_start = jnp.min(jnp.where(same_doc, row_index[None, :], rows_dev), axis=1)
    token_positions = (prefix_len + row_index - doc_start).astype(jnp.float32)
    normed_input = normalize(hidden_in).astype(jnp.bfloat16)
    query_rows_all = jnp.dot(normed_input, w_query, preferred_element_type=jnp.float32).reshape(
        rows_dev, kv_local * group_width, head_size
    )
    query_rows_all = (
        rotary_apply(query_rows_all, token_positions)
        .astype(jnp.bfloat16)
        .reshape(rows_dev, kv_local, group_width, head_size)
    )
    fresh_key = jnp.dot(normed_input, key_weight, preferred_element_type=jnp.float32).reshape(
        rows_dev, kv_local, head_size
    )
    fresh_key = rotary_apply(fresh_key, token_positions).astype(jnp.bfloat16)
    fresh_value = (
        jnp.dot(normed_input, value_weight, preferred_element_type=jnp.float32)
        .astype(jnp.bfloat16)
        .reshape(rows_dev, kv_local, head_size)
    )
    own_scores = (
        jnp.einsum("tkgd,skd->tkgs", query_rows_all, fresh_key, preferred_element_type=jnp.float32)
        / head_size
    )
    visible = same_doc & (row_index[None, :] <= row_index[:, None])
    own_scores = jnp.where(visible[:, None, None, :], own_scores, -jnp.inf)
    row_top = jnp.max(own_scores, axis=-1)
    weights = jnp.exp(own_scores - row_top[..., None])
    denominator = jnp.sum(weights, axis=-1)
    numerator = jnp.einsum(
        "tkgs,skd->tkgd",
        weights.astype(jnp.bfloat16),
        fresh_value,
        preferred_element_type=jnp.float32,
    )
    running = (row_top, denominator, numerator)
    prefix_both = jnp.concatenate([cached_prefix_keys, cached_prefix_values], axis=1)
    seq_total = prefix_len // prefix_both.shape[0]
    whole_both = lax.all_to_all(
        jnp.broadcast_to(prefix_both[None], (seq_total,) + prefix_both.shape), SEQ, 0, 0, tiled=True
    ).reshape(prefix_len, prefix_both.shape[1])
    top_old, denom_old, numer_old = running
    rows_q = rows_dev * group_width

    def heads_first(values):
        return jnp.swapaxes(values, 0, 1).reshape((kv_local, rows_q) + values.shape[3:])

    attended = prefix_attention(
        heads_first(query_rows_all),
        whole_both,
        heads_first(top_old[..., None]),
        heads_first(denom_old[..., None]),
        heads_first(numer_old),
        head_size,
    )
    attended = jnp.swapaxes(
        attended.reshape(kv_local, rows_dev, group_width, head_size), 0, 1
    ).reshape(rows_dev, kv_local * group_width * head_size)
    moe_rows = routes.shape[0]
    row_start = lax.axis_index("tp") * moe_rows
    attn_part = jnp.dot(attended, w_out, preferred_element_type=jnp.float32)
    tp_count = lax.axis_size("tp")
    exchanged = lax.all_to_all(
        attn_part.reshape(tp_count, moe_rows, column_list), "tp", 0, 0, tiled=True
    )
    attn_sum = jnp.sum(exchanged, axis=0)
    residual = (
        lax.dynamic_slice_in_dim(hidden_in, row_start, moe_rows, 0).astype(jnp.float32)
        + RESIDUAL * attn_sum
    )
    routed = normalize(residual).astype(jnp.bfloat16)
    experts = EXPERTS
    capacity = moe_rows // 2
    ff_part = expert_out.shape[1]
    onehot = (routes[:, :, None] == jnp.arange(experts, dtype=jnp.int32)[None, None, :]).astype(
        jnp.int32
    )
    per_row = jnp.sum(onehot, axis=1)
    before = jnp.cumsum(per_row, axis=0) - per_row
    rank_in = jnp.sum(onehot * before[:, None, :], axis=2)
    slot_of = routes * capacity + rank_in
    slot_ids = jnp.arange(experts * capacity, dtype=jnp.int32)
    pick_hit = slot_of[:, :, None] == slot_ids[None, None, :]
    selector = jnp.any(pick_hit, axis=1).T.astype(jnp.bfloat16)
    combiner = jnp.sum(jnp.where(pick_hit, gate_scores[:, :, None], 0.0), axis=1)
    gathered = jnp.dot(selector, routed, preferred_element_type=jnp.float32).astype(jnp.bfloat16)
    outgoing = gathered.reshape(experts, capacity, column_list)
    incoming = lax.all_to_all(outgoing, EXPERT_AXES, split_axis=0, concat_axis=0, tiled=True)
    incoming = incoming.reshape(experts * capacity, column_list)
    gate_up = jnp.einsum("rd,pdf->prf", incoming, full_in, preferred_element_type=jnp.float32)
    activated = (jax.nn.silu(gate_up[..., :ff_part]) * gate_up[..., ff_part:]).astype(jnp.bfloat16)
    partial_value = jnp.einsum(
        "prf,pfd->prd", activated, full_out, preferred_element_type=jnp.float32
    ).astype(jnp.bfloat16)
    part_total = jnp.sum(partial_value.astype(jnp.float32), axis=0).astype(jnp.bfloat16)
    returned = lax.all_to_all(
        part_total.reshape(experts, capacity, column_list), EXPERT_AXES, split_axis=0, concat_axis=0, tiled=True
    )
    part_sum = returned.reshape(experts * capacity, column_list).astype(jnp.float32)
    expert_sum = jnp.dot(
        combiner, part_sum, precision=lax.Precision.HIGHEST, preferred_element_type=jnp.float32
    )
    layer_out = (residual + RESIDUAL * expert_sum).astype(jnp.bfloat16)
    return (attn_sum.astype(jnp.bfloat16), expert_sum.astype(jnp.bfloat16), layer_out)


def solution(mesh):
    seq_size = mesh.shape["seq"]
    tp_size = mesh.shape["tp"]
    split = (seq_size // 16, 4, 2, 2, tp_size)
    fine_mesh = Mesh(mesh.devices.reshape(split), ("z", "yh", "yl", "c", "tp"))
    seq_spec = SEQ
    in_specs = (
        P(seq_spec, None),
        P(None, "tp"),
        P(None, "tp"),
        P(None, "tp"),
        P("tp", None),
        P(seq_spec, "tp"),
        P(seq_spec, "tp"),
        P(seq_spec, None),
        P(SEQ + ("tp",), None),
        P(SEQ + ("tp",), None),
        P(seq_spec, None, None),
        P(seq_spec, None, None),
    )
    out_specs = (P(SEQ + ("tp",), None),) * 3
    return jax.shard_map(body, mesh=fine_mesh, in_specs=in_specs, out_specs=out_specs, check_vma=False)
```

```python
import jax
import jax.numpy as jnp
from jax import lax
from jax.experimental import pallas as pl
from jax.sharding import Mesh, PartitionSpec as P

HEAD_WIDTH = 64
EXPERTS = 32


SEQ = ("z", "yh", "yl", "c")
EXPERT_AXES = ("z", "yh")
PART_AXES = ("yl", "c")
CHIP_AXES = ("z", "yh", "yl")
CORE_AXIS = "c"

EPSILON = 1e-06
RESIDUAL = 0.22


def normalize(values):
    values = values.astype(jnp.float32)
    return values * lax.rsqrt(jnp.mean(values * values, axis=-1, keepdims=True) + EPSILON)


def rotary_apply(values, token_positions):
    half_size = values.shape[-1] // 2
    frequency = jnp.exp(
        -jnp.log(10000.0) * jnp.arange(half_size, dtype=jnp.float32) * 2.0 / values.shape[-1]
    )
    angles = token_positions[:, None] * frequency[None, :]
    cosine = jnp.cos(angles)[:, None, :]
    sine_part = jnp.sin(angles)[:, None, :]
    first_half = values[..., :half_size]
    second = values[..., half_size:]
    return jnp.concatenate(
        [first_half * cosine - second * sine_part, second * cosine + first_half * sine_part],
        axis=-1,
    )


def prefix_attention(queries, keys_values, top_old, denom_old, numer_old, head_size):
    kv_local = queries.shape[0]
    value_base = keys_values.shape[1] // 2

    def kernel(q_ref, kv_ref, top_ref, den_ref, num_ref, out_ref):
        for head in range(kv_local):
            keys = kv_ref[:, head * head_size : (head + 1) * head_size]
            values = kv_ref[:, value_base + head * head_size : value_base + (head + 1) * head_size]
            scores = lax.dot_general(
                q_ref[head], keys, (((1,), (1,)), ((), ())), preferred_element_type=jnp.float32
            ) * (1.0 / head_size)
            top_prev = top_ref[head]
            top_new = jnp.maximum(top_prev, jnp.max(scores, axis=1, keepdims=True))
            shrink = jnp.exp(top_prev - top_new)
            weights = jnp.exp(scores - top_new)
            denom = den_ref[head] * shrink + jnp.sum(weights, axis=1, keepdims=True)
            numer = num_ref[head] * shrink + jnp.dot(
                weights.astype(jnp.bfloat16), values, preferred_element_type=jnp.float32
            )
            out_ref[head] = (numer / denom).astype(jnp.bfloat16)

    return pl.pallas_call(
        kernel, out_shape=jax.ShapeDtypeStruct(queries.shape, jnp.bfloat16)
    )(queries, keys_values, top_old, denom_old, numer_old)


def body(
    hidden_in,
    w_query,
    key_weight,
    value_weight,
    w_out,
    cached_prefix_keys,
    cached_prefix_values,
    doc_ids,
    routes,
    gate_scores,
    expert_in,
    expert_out,
):
    in_cols = expert_in.shape[2]
    packed = jnp.concatenate(
        [expert_in, expert_out.reshape(expert_out.shape[0], expert_in.shape[1], -1)], axis=2
    )
    packed = lax.all_gather(packed, PART_AXES, axis=0, tiled=True)
    full_in = packed[..., :in_cols]
    full_out = packed[..., in_cols:].reshape((packed.shape[0],) + expert_out.shape[1:])
    rows_dev = hidden_in.shape[0]
    column_list = hidden_in.shape[1]
    head_size = HEAD_WIDTH
    kv_local = key_weight.shape[1] // head_size
    group_width = w_query.shape[1] // head_size // kv_local
    seq_count = lax.axis_size(SEQ)
    prefix_len = cached_prefix_keys.shape[0] * seq_count
    doc_row = doc_ids[0]
    row_index = jnp.arange(rows_dev, dtype=jnp.int32)
    same_doc = doc_row[:, None] == doc_row[None, :]
    doc_start = jnp.min(jnp.where(same_doc, row_index[None, :], rows_dev), axis=1)
    token_positions = (prefix_len + row_index - doc_start).astype(jnp.float32)
    normed_input = normalize(hidden_in).astype(jnp.bfloat16)
    query_rows_all = jnp.dot(normed_input, w_query, preferred_element_type=jnp.float32).reshape(
        rows_dev, kv_local * group_width, head_size
    )
    query_rows_all = (
        rotary_apply(query_rows_all, token_positions)
        .astype(jnp.bfloat16)
        .reshape(rows_dev, kv_local, group_width, head_size)
    )
    fresh_key = jnp.dot(normed_input, key_weight, preferred_element_type=jnp.float32).reshape(
        rows_dev, kv_local, head_size
    )
    fresh_key = rotary_apply(fresh_key, token_positions).astype(jnp.bfloat16)
    fresh_value = (
        jnp.dot(normed_input, value_weight, preferred_element_type=jnp.float32)
        .astype(jnp.bfloat16)
        .reshape(rows_dev, kv_local, head_size)
    )
    own_scores = (
        jnp.einsum("tkgd,skd->tkgs", query_rows_all, fresh_key, preferred_element_type=jnp.float32)
        / head_size
    )
    visible = same_doc & (row_index[None, :] <= row_index[:, None])
    own_scores = jnp.where(visible[:, None, None, :], own_scores, -jnp.inf)
    row_top = jnp.max(own_scores, axis=-1)
    weights = jnp.exp(own_scores - row_top[..., None])
    denominator = jnp.sum(weights, axis=-1)
    numerator = jnp.einsum(
        "tkgs,skd->tkgd",
        weights.astype(jnp.bfloat16),
        fresh_value,
        preferred_element_type=jnp.float32,
    )
    running = (row_top, denominator, numerator)
    prefix_both = jnp.concatenate([cached_prefix_keys, cached_prefix_values], axis=1)
    chip_total = prefix_len // prefix_both.shape[0] // lax.axis_size(CORE_AXIS)
    same_core = lax.all_to_all(
        jnp.broadcast_to(prefix_both[None], (chip_total,) + prefix_both.shape), CHIP_AXES, 0, 0, tiled=True
    ).reshape(-1, prefix_both.shape[1])
    other_core = lax.ppermute(same_core, CORE_AXIS, [(0, 1), (1, 0)])
    whole_both = jnp.concatenate([same_core, other_core], axis=0)
    top_old, denom_old, numer_old = running
    rows_q = rows_dev * group_width

    def heads_first(values):
        return jnp.swapaxes(values, 0, 1).reshape((kv_local, rows_q) + values.shape[3:])

    attended = prefix_attention(
        heads_first(query_rows_all),
        whole_both,
        heads_first(top_old[..., None]),
        heads_first(denom_old[..., None]),
        heads_first(numer_old),
        head_size,
    )
    attended = jnp.swapaxes(
        attended.reshape(kv_local, rows_dev, group_width, head_size), 0, 1
    ).reshape(rows_dev, kv_local * group_width * head_size)
    moe_rows = routes.shape[0]
    row_start = lax.axis_index("tp") * moe_rows
    attn_part = jnp.dot(attended, w_out, preferred_element_type=jnp.float32)
    tp_count = lax.axis_size("tp")
    exchanged = lax.all_to_all(
        attn_part.reshape(tp_count, moe_rows, column_list), "tp", 0, 0, tiled=True
    )
    attn_sum = jnp.sum(exchanged, axis=0)
    residual = (
        lax.dynamic_slice_in_dim(hidden_in, row_start, moe_rows, 0).astype(jnp.float32)
        + RESIDUAL * attn_sum
    )
    routed = normalize(residual).astype(jnp.bfloat16)
    experts = EXPERTS
    capacity = moe_rows // 2
    ff_part = expert_out.shape[1]
    onehot = (routes[:, :, None] == jnp.arange(experts, dtype=jnp.int32)[None, None, :]).astype(
        jnp.int32
    )
    per_row = jnp.sum(onehot, axis=1)
    before = jnp.cumsum(per_row, axis=0) - per_row
    rank_in = jnp.sum(onehot * before[:, None, :], axis=2)
    slot_of = routes * capacity + rank_in
    slot_ids = jnp.arange(experts * capacity, dtype=jnp.int32)
    pick_hit = slot_of[:, :, None] == slot_ids[None, None, :]
    selector = jnp.any(pick_hit, axis=1).T.astype(jnp.bfloat16)
    combiner = jnp.sum(jnp.where(pick_hit, gate_scores[:, :, None], 0.0), axis=1)
    gathered = jnp.dot(selector, routed, preferred_element_type=jnp.float32).astype(jnp.bfloat16)
    outgoing = gathered.reshape(experts, capacity, column_list)
    incoming = lax.all_to_all(outgoing, EXPERT_AXES, split_axis=0, concat_axis=0, tiled=True)
    incoming = incoming.reshape(experts * capacity, column_list)
    gate_up = jnp.einsum("rd,pdf->prf", incoming, full_in, preferred_element_type=jnp.float32)
    activated = (jax.nn.silu(gate_up[..., :ff_part]) * gate_up[..., ff_part:]).astype(jnp.bfloat16)
    partial_value = jnp.einsum(
        "prf,pfd->prd", activated, full_out, preferred_element_type=jnp.float32
    ).astype(jnp.bfloat16)
    part_total = jnp.sum(partial_value.astype(jnp.float32), axis=0).astype(jnp.bfloat16)
    returned = lax.all_to_all(
        part_total.reshape(experts, capacity, column_list), EXPERT_AXES, split_axis=0, concat_axis=0, tiled=True
    )
    part_sum = returned.reshape(experts * capacity, column_list).astype(jnp.float32)
    expert_sum = jnp.dot(
        combiner, part_sum, precision=lax.Precision.HIGHEST, preferred_element_type=jnp.float32
    )
    layer_out = (residual + RESIDUAL * expert_sum).astype(jnp.bfloat16)
    return (attn_sum.astype(jnp.bfloat16), expert_sum.astype(jnp.bfloat16), layer_out)


def solution(mesh):
    seq_size = mesh.shape["seq"]
    tp_size = mesh.shape["tp"]
    split = (seq_size // 16, 4, 2, 2, tp_size)
    fine_mesh = Mesh(mesh.devices.reshape(split), ("z", "yh", "yl", "c", "tp"))
    seq_spec = SEQ
    in_specs = (
        P(seq_spec, None),
        P(None, "tp"),
        P(None, "tp"),
        P(None, "tp"),
        P("tp", None),
        P(seq_spec, "tp"),
        P(seq_spec, "tp"),
        P(seq_spec, None),
        P(SEQ + ("tp",), None),
        P(SEQ + ("tp",), None),
        P(seq_spec, None, None),
        P(seq_spec, None, None),
    )
    out_specs = (P(SEQ + ("tp",), None),) * 3
    return jax.shard_map(body, mesh=fine_mesh, in_specs=in_specs, out_specs=out_specs, check_vma=False)
```

```python
import jax
import jax.numpy as jnp
from jax import lax
from jax.experimental import pallas as pl
from jax.sharding import Mesh, PartitionSpec as P

HEAD_WIDTH = 64
EXPERTS = 32


SEQ = ("z", "yh", "yl", "c")
EXPERT_AXES = ("z", "yh")
PART_AXES = ("yl", "c")
CHIP_AXES = ("z", "yh", "yl")
CORE_AXIS = "c"

EPSILON = 1e-06
RESIDUAL = 0.22


def normalize(values):
    values = values.astype(jnp.float32)
    return values * lax.rsqrt(jnp.mean(values * values, axis=-1, keepdims=True) + EPSILON)


def rotary_apply(values, token_positions):
    half_size = values.shape[-1] // 2
    frequency = jnp.exp(
        -jnp.log(10000.0) * jnp.arange(half_size, dtype=jnp.float32) * 2.0 / values.shape[-1]
    )
    angles = token_positions[:, None] * frequency[None, :]
    cosine = jnp.cos(angles)[:, None, :]
    sine_part = jnp.sin(angles)[:, None, :]
    first_half = values[..., :half_size]
    second = values[..., half_size:]
    return jnp.concatenate(
        [first_half * cosine - second * sine_part, second * cosine + first_half * sine_part],
        axis=-1,
    )


def prefix_attention(queries, keys_values, top_old, denom_old, numer_old, head_size):
    kv_local = queries.shape[0]
    value_base = keys_values.shape[1] // 2

    def kernel(q_ref, kv_ref, top_ref, den_ref, num_ref, out_ref):
        for head in range(kv_local):
            keys = kv_ref[:, head * head_size : (head + 1) * head_size]
            values = kv_ref[:, value_base + head * head_size : value_base + (head + 1) * head_size]
            scores = lax.dot_general(
                q_ref[head], keys, (((1,), (1,)), ((), ())), preferred_element_type=jnp.float32
            ) * (1.0 / head_size)
            top_prev = top_ref[head]
            top_new = jnp.maximum(top_prev, jnp.max(scores, axis=1, keepdims=True))
            shrink = jnp.exp(top_prev - top_new)
            weights = jnp.exp(scores - top_new)
            denom = den_ref[head] * shrink + jnp.sum(weights, axis=1, keepdims=True)
            numer = num_ref[head] * shrink + jnp.dot(
                weights.astype(jnp.bfloat16), values, preferred_element_type=jnp.float32
            )
            out_ref[head] = (numer / denom).astype(jnp.bfloat16)

    return pl.pallas_call(
        kernel, out_shape=jax.ShapeDtypeStruct(queries.shape, jnp.bfloat16)
    )(queries, keys_values, top_old, denom_old, numer_old)


def body(
    hidden_in,
    w_query,
    key_weight,
    value_weight,
    w_out,
    cached_prefix_keys,
    cached_prefix_values,
    doc_ids,
    routes,
    gate_scores,
    expert_in,
    expert_out,
):
    in_cols = expert_in.shape[2]
    packed = jnp.concatenate(
        [expert_in, expert_out.reshape(expert_out.shape[0], expert_in.shape[1], -1)], axis=2
    )
    packed = lax.all_gather(packed, PART_AXES[0], axis=0, tiled=True)
    packed = lax.all_gather(packed, PART_AXES[1], axis=0, tiled=True)
    full_in = packed[..., :in_cols]
    full_out = packed[..., in_cols:].reshape((packed.shape[0],) + expert_out.shape[1:])
    rows_dev = hidden_in.shape[0]
    column_list = hidden_in.shape[1]
    head_size = HEAD_WIDTH
    kv_local = key_weight.shape[1] // head_size
    group_width = w_query.shape[1] // head_size // kv_local
    seq_count = lax.axis_size(SEQ)
    prefix_len = cached_prefix_keys.shape[0] * seq_count
    doc_row = doc_ids[0]
    row_index = jnp.arange(rows_dev, dtype=jnp.int32)
    same_doc = doc_row[:, None] == doc_row[None, :]
    doc_start = jnp.min(jnp.where(same_doc, row_index[None, :], rows_dev), axis=1)
    token_positions = (prefix_len + row_index - doc_start).astype(jnp.float32)
    normed_input = normalize(hidden_in).astype(jnp.bfloat16)
    query_rows_all = jnp.dot(normed_input, w_query, preferred_element_type=jnp.float32).reshape(
        rows_dev, kv_local * group_width, head_size
    )
    query_rows_all = (
        rotary_apply(query_rows_all, token_positions)
        .astype(jnp.bfloat16)
        .reshape(rows_dev, kv_local, group_width, head_size)
    )
    fresh_key = jnp.dot(normed_input, key_weight, preferred_element_type=jnp.float32).reshape(
        rows_dev, kv_local, head_size
    )
    fresh_key = rotary_apply(fresh_key, token_positions).astype(jnp.bfloat16)
    fresh_value = (
        jnp.dot(normed_input, value_weight, preferred_element_type=jnp.float32)
        .astype(jnp.bfloat16)
        .reshape(rows_dev, kv_local, head_size)
    )
    own_scores = (
        jnp.einsum("tkgd,skd->tkgs", query_rows_all, fresh_key, preferred_element_type=jnp.float32)
        / head_size
    )
    visible = same_doc & (row_index[None, :] <= row_index[:, None])
    own_scores = jnp.where(visible[:, None, None, :], own_scores, -jnp.inf)
    row_top = jnp.max(own_scores, axis=-1)
    weights = jnp.exp(own_scores - row_top[..., None])
    denominator = jnp.sum(weights, axis=-1)
    numerator = jnp.einsum(
        "tkgs,skd->tkgd",
        weights.astype(jnp.bfloat16),
        fresh_value,
        preferred_element_type=jnp.float32,
    )
    running = (row_top, denominator, numerator)
    prefix_both = jnp.concatenate([cached_prefix_keys, cached_prefix_values], axis=1)
    chip_total = prefix_len // prefix_both.shape[0] // lax.axis_size(CORE_AXIS)
    same_core = lax.all_to_all(
        jnp.broadcast_to(prefix_both[None], (chip_total,) + prefix_both.shape), CHIP_AXES, 0, 0, tiled=True
    ).reshape(-1, prefix_both.shape[1])
    other_core = lax.ppermute(same_core, CORE_AXIS, [(0, 1), (1, 0)])
    whole_both = jnp.concatenate([same_core, other_core], axis=0)
    top_old, denom_old, numer_old = running
    rows_q = rows_dev * group_width

    def heads_first(values):
        return jnp.swapaxes(values, 0, 1).reshape((kv_local, rows_q) + values.shape[3:])

    attended = prefix_attention(
        heads_first(query_rows_all),
        whole_both,
        heads_first(top_old[..., None]),
        heads_first(denom_old[..., None]),
        heads_first(numer_old),
        head_size,
    )
    attended = jnp.swapaxes(
        attended.reshape(kv_local, rows_dev, group_width, head_size), 0, 1
    ).reshape(rows_dev, kv_local * group_width * head_size)
    moe_rows = routes.shape[0]
    row_start = lax.axis_index("tp") * moe_rows
    attn_part = jnp.dot(attended, w_out, preferred_element_type=jnp.float32)
    tp_count = lax.axis_size("tp")
    exchanged = lax.all_to_all(
        attn_part.reshape(tp_count, moe_rows, column_list), "tp", 0, 0, tiled=True
    )
    attn_sum = jnp.sum(exchanged, axis=0)
    residual = (
        lax.dynamic_slice_in_dim(hidden_in, row_start, moe_rows, 0).astype(jnp.float32)
        + RESIDUAL * attn_sum
    )
    routed = normalize(residual).astype(jnp.bfloat16)
    experts = EXPERTS
    capacity = moe_rows // 2
    ff_part = expert_out.shape[1]
    onehot = (routes[:, :, None] == jnp.arange(experts, dtype=jnp.int32)[None, None, :]).astype(
        jnp.int32
    )
    per_row = jnp.sum(onehot, axis=1)
    before = jnp.cumsum(per_row, axis=0) - per_row
    rank_in = jnp.sum(onehot * before[:, None, :], axis=2)
    slot_of = routes * capacity + rank_in
    slot_ids = jnp.arange(experts * capacity, dtype=jnp.int32)
    pick_hit = slot_of[:, :, None] == slot_ids[None, None, :]
    selector = jnp.any(pick_hit, axis=1).T.astype(jnp.bfloat16)
    combiner = jnp.sum(jnp.where(pick_hit, gate_scores[:, :, None], 0.0), axis=1)
    gathered = jnp.dot(selector, routed, preferred_element_type=jnp.float32).astype(jnp.bfloat16)
    outgoing = gathered.reshape(experts, capacity, column_list)
    incoming = lax.all_to_all(outgoing, EXPERT_AXES, split_axis=0, concat_axis=0, tiled=True)
    incoming = incoming.reshape(experts * capacity, column_list)
    gate_up = jnp.einsum("rd,pdf->prf", incoming, full_in, preferred_element_type=jnp.float32)
    activated = (jax.nn.silu(gate_up[..., :ff_part]) * gate_up[..., ff_part:]).astype(jnp.bfloat16)
    partial_value = jnp.einsum(
        "prf,pfd->prd", activated, full_out, preferred_element_type=jnp.float32
    ).astype(jnp.bfloat16)
    part_total = jnp.sum(partial_value.astype(jnp.float32), axis=0).astype(jnp.bfloat16)
    returned = lax.all_to_all(
        part_total.reshape(experts, capacity, column_list), EXPERT_AXES, split_axis=0, concat_axis=0, tiled=True
    )
    part_sum = returned.reshape(experts * capacity, column_list).astype(jnp.float32)
    expert_sum = jnp.dot(
        combiner, part_sum, precision=lax.Precision.HIGHEST, preferred_element_type=jnp.float32
    )
    layer_out = (residual + RESIDUAL * expert_sum).astype(jnp.bfloat16)
    return (attn_sum.astype(jnp.bfloat16), expert_sum.astype(jnp.bfloat16), layer_out)


def solution(mesh):
    seq_size = mesh.shape["seq"]
    tp_size = mesh.shape["tp"]
    split = (seq_size // 16, 4, 2, 2, tp_size)
    fine_mesh = Mesh(mesh.devices.reshape(split), ("z", "yh", "yl", "c", "tp"))
    seq_spec = SEQ
    in_specs = (
        P(seq_spec, None),
        P(None, "tp"),
        P(None, "tp"),
        P(None, "tp"),
        P("tp", None),
        P(seq_spec, "tp"),
        P(seq_spec, "tp"),
        P(seq_spec, None),
        P(SEQ + ("tp",), None),
        P(SEQ + ("tp",), None),
        P(seq_spec, None, None),
        P(seq_spec, None, None),
    )
    out_specs = (P(SEQ + ("tp",), None),) * 3
    return jax.shard_map(body, mesh=fine_mesh, in_specs=in_specs, out_specs=out_specs, check_vma=False)
```

```python
import jax
import jax.numpy as jnp
from jax import lax
from jax.experimental import pallas as pl
from jax.sharding import Mesh, PartitionSpec as P

HEAD_WIDTH = 64
EXPERTS = 32


SEQ = ("z", "yh", "yl", "c")
EXPERT_AXES = ("z", "yh")
PART_AXES = ("yl", "c")
CHIP_AXES = ("z", "yh", "yl")
CORE_AXIS = "c"

EPSILON = 1e-06
RESIDUAL = 0.22


def normalize(values):
    values = values.astype(jnp.float32)
    return values * lax.rsqrt(jnp.mean(values * values, axis=-1, keepdims=True) + EPSILON)


def rotary_apply(values, token_positions):
    half_size = values.shape[-1] // 2
    frequency = jnp.exp(
        -jnp.log(10000.0) * jnp.arange(half_size, dtype=jnp.float32) * 2.0 / values.shape[-1]
    )
    angles = token_positions[:, None] * frequency[None, :]
    cosine = jnp.cos(angles)[:, None, :]
    sine_part = jnp.sin(angles)[:, None, :]
    first_half = values[..., :half_size]
    second = values[..., half_size:]
    return jnp.concatenate(
        [first_half * cosine - second * sine_part, second * cosine + first_half * sine_part],
        axis=-1,
    )


def prefix_attention(queries, keys_values, top_old, denom_old, numer_old, head_size):
    kv_local = queries.shape[0]
    value_base = keys_values.shape[1] // 2

    def kernel(q_ref, kv_ref, top_ref, den_ref, num_ref, out_ref):
        for head in range(kv_local):
            keys = kv_ref[:, head * head_size : (head + 1) * head_size]
            values = kv_ref[:, value_base + head * head_size : value_base + (head + 1) * head_size]
            scores = lax.dot_general(
                q_ref[head], keys, (((1,), (1,)), ((), ())), preferred_element_type=jnp.float32
            ) * (1.0 / head_size)
            top_prev = top_ref[head]
            top_new = jnp.maximum(top_prev, jnp.max(scores, axis=1, keepdims=True))
            shrink = jnp.exp(top_prev - top_new)
            weights = jnp.exp(scores - top_new)
            denom = den_ref[head] * shrink + jnp.sum(weights, axis=1, keepdims=True)
            numer = num_ref[head] * shrink + jnp.dot(
                weights.astype(jnp.bfloat16), values, preferred_element_type=jnp.float32
            )
            out_ref[head] = (numer / denom).astype(jnp.bfloat16)

    return pl.pallas_call(
        kernel, out_shape=jax.ShapeDtypeStruct(queries.shape, jnp.bfloat16)
    )(queries, keys_values, top_old, denom_old, numer_old)


def body(
    hidden_in,
    w_query,
    key_weight,
    value_weight,
    w_out,
    cached_prefix_keys,
    cached_prefix_values,
    doc_ids,
    routes,
    gate_scores,
    expert_in,
    expert_out,
):
    in_cols = expert_in.shape[2]
    packed = jnp.concatenate(
        [expert_in, expert_out.reshape(expert_out.shape[0], expert_in.shape[1], -1)], axis=2
    )
    packed = lax.all_gather(packed, PART_AXES[0], axis=0, tiled=True)
    packed = jnp.concatenate([packed, lax.ppermute(packed, CORE_AXIS, [(0, 1), (1, 0)])], axis=0)
    full_in = packed[..., :in_cols]
    full_out = packed[..., in_cols:].reshape((packed.shape[0],) + expert_out.shape[1:])
    rows_dev = hidden_in.shape[0]
    column_list = hidden_in.shape[1]
    head_size = HEAD_WIDTH
    kv_local = key_weight.shape[1] // head_size
    group_width = w_query.shape[1] // head_size // kv_local
    seq_count = lax.axis_size(SEQ)
    prefix_len = cached_prefix_keys.shape[0] * seq_count
    doc_row = doc_ids[0]
    row_index = jnp.arange(rows_dev, dtype=jnp.int32)
    same_doc = doc_row[:, None] == doc_row[None, :]
    doc_start = jnp.min(jnp.where(same_doc, row_index[None, :], rows_dev), axis=1)
    token_positions = (prefix_len + row_index - doc_start).astype(jnp.float32)
    normed_input = normalize(hidden_in).astype(jnp.bfloat16)
    query_rows_all = jnp.dot(normed_input, w_query, preferred_element_type=jnp.float32).reshape(
        rows_dev, kv_local * group_width, head_size
    )
    query_rows_all = (
        rotary_apply(query_rows_all, token_positions)
        .astype(jnp.bfloat16)
        .reshape(rows_dev, kv_local, group_width, head_size)
    )
    fresh_key = jnp.dot(normed_input, key_weight, preferred_element_type=jnp.float32).reshape(
        rows_dev, kv_local, head_size
    )
    fresh_key = rotary_apply(fresh_key, token_positions).astype(jnp.bfloat16)
    fresh_value = (
        jnp.dot(normed_input, value_weight, preferred_element_type=jnp.float32)
        .astype(jnp.bfloat16)
        .reshape(rows_dev, kv_local, head_size)
    )
    own_scores = (
        jnp.einsum("tkgd,skd->tkgs", query_rows_all, fresh_key, preferred_element_type=jnp.float32)
        / head_size
    )
    visible = same_doc & (row_index[None, :] <= row_index[:, None])
    own_scores = jnp.where(visible[:, None, None, :], own_scores, -jnp.inf)
    row_top = jnp.max(own_scores, axis=-1)
    weights = jnp.exp(own_scores - row_top[..., None])
    denominator = jnp.sum(weights, axis=-1)
    numerator = jnp.einsum(
        "tkgs,skd->tkgd",
        weights.astype(jnp.bfloat16),
        fresh_value,
        preferred_element_type=jnp.float32,
    )
    running = (row_top, denominator, numerator)
    prefix_both = jnp.concatenate([cached_prefix_keys, cached_prefix_values], axis=1)
    chip_total = prefix_len // prefix_both.shape[0] // lax.axis_size(CORE_AXIS)
    same_core = lax.all_to_all(
        jnp.broadcast_to(prefix_both[None], (chip_total,) + prefix_both.shape), CHIP_AXES, 0, 0, tiled=True
    ).reshape(-1, prefix_both.shape[1])
    other_core = lax.ppermute(same_core, CORE_AXIS, [(0, 1), (1, 0)])
    whole_both = jnp.concatenate([same_core, other_core], axis=0)
    top_old, denom_old, numer_old = running
    rows_q = rows_dev * group_width

    def heads_first(values):
        return jnp.swapaxes(values, 0, 1).reshape((kv_local, rows_q) + values.shape[3:])

    attended = prefix_attention(
        heads_first(query_rows_all),
        whole_both,
        heads_first(top_old[..., None]),
        heads_first(denom_old[..., None]),
        heads_first(numer_old),
        head_size,
    )
    attended = jnp.swapaxes(
        attended.reshape(kv_local, rows_dev, group_width, head_size), 0, 1
    ).reshape(rows_dev, kv_local * group_width * head_size)
    moe_rows = routes.shape[0]
    row_start = lax.axis_index("tp") * moe_rows
    attn_part = jnp.dot(attended, w_out, preferred_element_type=jnp.float32)
    tp_count = lax.axis_size("tp")
    exchanged = lax.all_to_all(
        attn_part.reshape(tp_count, moe_rows, column_list), "tp", 0, 0, tiled=True
    )
    attn_sum = jnp.sum(exchanged, axis=0)
    residual = (
        lax.dynamic_slice_in_dim(hidden_in, row_start, moe_rows, 0).astype(jnp.float32)
        + RESIDUAL * attn_sum
    )
    routed = normalize(residual).astype(jnp.bfloat16)
    experts = EXPERTS
    capacity = moe_rows // 2
    ff_part = expert_out.shape[1]
    onehot = (routes[:, :, None] == jnp.arange(experts, dtype=jnp.int32)[None, None, :]).astype(
        jnp.int32
    )
    per_row = jnp.sum(onehot, axis=1)
    before = jnp.cumsum(per_row, axis=0) - per_row
    rank_in = jnp.sum(onehot * before[:, None, :], axis=2)
    slot_of = routes * capacity + rank_in
    slot_ids = jnp.arange(experts * capacity, dtype=jnp.int32)
    pick_hit = slot_of[:, :, None] == slot_ids[None, None, :]
    selector = jnp.any(pick_hit, axis=1).T.astype(jnp.bfloat16)
    combiner = jnp.sum(jnp.where(pick_hit, gate_scores[:, :, None], 0.0), axis=1)
    gathered = jnp.dot(selector, routed, preferred_element_type=jnp.float32).astype(jnp.bfloat16)
    outgoing = gathered.reshape(experts, capacity, column_list)
    incoming = lax.all_to_all(outgoing, EXPERT_AXES, split_axis=0, concat_axis=0, tiled=True)
    incoming = incoming.reshape(experts * capacity, column_list)
    gate_up = jnp.einsum("rd,pdf->prf", incoming, full_in, preferred_element_type=jnp.float32)
    activated = (jax.nn.silu(gate_up[..., :ff_part]) * gate_up[..., ff_part:]).astype(jnp.bfloat16)
    partial_value = jnp.einsum(
        "prf,pfd->prd", activated, full_out, preferred_element_type=jnp.float32
    ).astype(jnp.bfloat16)
    part_total = jnp.sum(partial_value.astype(jnp.float32), axis=0).astype(jnp.bfloat16)
    returned = lax.all_to_all(
        part_total.reshape(experts, capacity, column_list), EXPERT_AXES, split_axis=0, concat_axis=0, tiled=True
    )
    part_sum = returned.reshape(experts * capacity, column_list).astype(jnp.float32)
    expert_sum = jnp.dot(
        combiner, part_sum, precision=lax.Precision.HIGHEST, preferred_element_type=jnp.float32
    )
    layer_out = (residual + RESIDUAL * expert_sum).astype(jnp.bfloat16)
    return (attn_sum.astype(jnp.bfloat16), expert_sum.astype(jnp.bfloat16), layer_out)


def solution(mesh):
    seq_size = mesh.shape["seq"]
    tp_size = mesh.shape["tp"]
    split = (seq_size // 16, 4, 2, 2, tp_size)
    fine_mesh = Mesh(mesh.devices.reshape(split), ("z", "yh", "yl", "c", "tp"))
    seq_spec = SEQ
    in_specs = (
        P(seq_spec, None),
        P(None, "tp"),
        P(None, "tp"),
        P(None, "tp"),
        P("tp", None),
        P(seq_spec, "tp"),
        P(seq_spec, "tp"),
        P(seq_spec, None),
        P(SEQ + ("tp",), None),
        P(SEQ + ("tp",), None),
        P(seq_spec, None, None),
        P(seq_spec, None, None),
    )
    out_specs = (P(SEQ + ("tp",), None),) * 3
    return jax.shard_map(body, mesh=fine_mesh, in_specs=in_specs, out_specs=out_specs, check_vma=False)
```

```python
import jax
import jax.numpy as jnp
from jax import lax
from jax.experimental import pallas as pl
from jax.sharding import Mesh, PartitionSpec as P

HEAD_WIDTH = 64
EXPERTS = 32


SEQ = ("z", "yh", "yl", "c")
EXPERT_AXES = ("z", "yh")
PART_AXES = ("yl", "c")
CHIP_AXES = ("z", "yh", "yl")
CORE_AXIS = "c"

EPSILON = 1e-06
RESIDUAL = 0.22


def normalize(values):
    values = values.astype(jnp.float32)
    return values * lax.rsqrt(jnp.mean(values * values, axis=-1, keepdims=True) + EPSILON)


def rotary_apply(values, token_positions):
    half_size = values.shape[-1] // 2
    frequency = jnp.exp(
        -jnp.log(10000.0) * jnp.arange(half_size, dtype=jnp.float32) * 2.0 / values.shape[-1]
    )
    angles = token_positions[:, None] * frequency[None, :]
    cosine = jnp.cos(angles)[:, None, :]
    sine_part = jnp.sin(angles)[:, None, :]
    first_half = values[..., :half_size]
    second = values[..., half_size:]
    return jnp.concatenate(
        [first_half * cosine - second * sine_part, second * cosine + first_half * sine_part],
        axis=-1,
    )


def prefix_attention(queries, kv_halves, top_old, denom_old, numer_old, head_size):
    kv_local = queries.shape[0]
    value_base = kv_halves[0].shape[1] // 2
    halves = len(kv_halves)

    def kernel(q_ref, *refs):
        kv_refs = refs[:halves]
        top_ref, den_ref, num_ref, out_ref = refs[halves:]
        for head in range(kv_local):
            key_cols = slice(head * head_size, (head + 1) * head_size)
            value_cols = slice(value_base + head * head_size, value_base + (head + 1) * head_size)
            scores = [
                lax.dot_general(
                    q_ref[head], kv_ref[:, key_cols], (((1,), (1,)), ((), ())),
                    preferred_element_type=jnp.float32,
                ) * (1.0 / head_size)
                for kv_ref in kv_refs
            ]
            top_prev = top_ref[head]
            top_new = top_prev
            for part in scores:
                top_new = jnp.maximum(top_new, jnp.max(part, axis=1, keepdims=True))
            shrink = jnp.exp(top_prev - top_new)
            denom = den_ref[head] * shrink
            numer = num_ref[head] * shrink
            for part, kv_ref in zip(scores, kv_refs):
                weights = jnp.exp(part - top_new)
                denom = denom + jnp.sum(weights, axis=1, keepdims=True)
                numer = numer + jnp.dot(
                    weights.astype(jnp.bfloat16), kv_ref[:, value_cols], preferred_element_type=jnp.float32
                )
            out_ref[head] = (numer / denom).astype(jnp.bfloat16)

    return pl.pallas_call(
        kernel, out_shape=jax.ShapeDtypeStruct(queries.shape, jnp.bfloat16)
    )(queries, *kv_halves, top_old, denom_old, numer_old)


def body(
    hidden_in,
    w_query,
    key_weight,
    value_weight,
    w_out,
    cached_prefix_keys,
    cached_prefix_values,
    doc_ids,
    routes,
    gate_scores,
    expert_in,
    expert_out,
):
    in_cols = expert_in.shape[2]
    packed = jnp.concatenate(
        [expert_in, expert_out.reshape(expert_out.shape[0], expert_in.shape[1], -1)], axis=2
    )
    packed = lax.all_gather(packed, PART_AXES, axis=0, tiled=True)
    full_in = packed[..., :in_cols]
    full_out = packed[..., in_cols:].reshape((packed.shape[0],) + expert_out.shape[1:])
    rows_dev = hidden_in.shape[0]
    column_list = hidden_in.shape[1]
    head_size = HEAD_WIDTH
    kv_local = key_weight.shape[1] // head_size
    group_width = w_query.shape[1] // head_size // kv_local
    seq_count = lax.axis_size(SEQ)
    prefix_len = cached_prefix_keys.shape[0] * seq_count
    doc_row = doc_ids[0]
    row_index = jnp.arange(rows_dev, dtype=jnp.int32)
    same_doc = doc_row[:, None] == doc_row[None, :]
    doc_start = jnp.min(jnp.where(same_doc, row_index[None, :], rows_dev), axis=1)
    token_positions = (prefix_len + row_index - doc_start).astype(jnp.float32)
    normed_input = normalize(hidden_in).astype(jnp.bfloat16)
    query_rows_all = jnp.dot(normed_input, w_query, preferred_element_type=jnp.float32).reshape(
        rows_dev, kv_local * group_width, head_size
    )
    query_rows_all = (
        rotary_apply(query_rows_all, token_positions)
        .astype(jnp.bfloat16)
        .reshape(rows_dev, kv_local, group_width, head_size)
    )
    fresh_key = jnp.dot(normed_input, key_weight, preferred_element_type=jnp.float32).reshape(
        rows_dev, kv_local, head_size
    )
    fresh_key = rotary_apply(fresh_key, token_positions).astype(jnp.bfloat16)
    fresh_value = (
        jnp.dot(normed_input, value_weight, preferred_element_type=jnp.float32)
        .astype(jnp.bfloat16)
        .reshape(rows_dev, kv_local, head_size)
    )
    own_scores = (
        jnp.einsum("tkgd,skd->tkgs", query_rows_all, fresh_key, preferred_element_type=jnp.float32)
        / head_size
    )
    visible = same_doc & (row_index[None, :] <= row_index[:, None])
    own_scores = jnp.where(visible[:, None, None, :], own_scores, -jnp.inf)
    row_top = jnp.max(own_scores, axis=-1)
    weights = jnp.exp(own_scores - row_top[..., None])
    denominator = jnp.sum(weights, axis=-1)
    numerator = jnp.einsum(
        "tkgs,skd->tkgd",
        weights.astype(jnp.bfloat16),
        fresh_value,
        preferred_element_type=jnp.float32,
    )
    running = (row_top, denominator, numerator)
    prefix_both = jnp.concatenate([cached_prefix_keys, cached_prefix_values], axis=1)
    chip_total = prefix_len // prefix_both.shape[0] // lax.axis_size(CORE_AXIS)
    same_core = lax.all_to_all(
        jnp.broadcast_to(prefix_both[None], (chip_total,) + prefix_both.shape), CHIP_AXES, 0, 0, tiled=True
    ).reshape(-1, prefix_both.shape[1])
    other_core = lax.ppermute(same_core, CORE_AXIS, [(0, 1), (1, 0)])
    top_old, denom_old, numer_old = running
    rows_q = rows_dev * group_width

    def heads_first(values):
        return jnp.swapaxes(values, 0, 1).reshape((kv_local, rows_q) + values.shape[3:])

    attended = prefix_attention(
        heads_first(query_rows_all),
        (same_core, other_core),
        heads_first(top_old[..., None]),
        heads_first(denom_old[..., None]),
        heads_first(numer_old),
        head_size,
    )
    attended = jnp.swapaxes(
        attended.reshape(kv_local, rows_dev, group_width, head_size), 0, 1
    ).reshape(rows_dev, kv_local * group_width * head_size)
    moe_rows = routes.shape[0]
    row_start = lax.axis_index("tp") * moe_rows
    attn_part = jnp.dot(attended, w_out, preferred_element_type=jnp.float32)
    tp_count = lax.axis_size("tp")
    exchanged = lax.all_to_all(
        attn_part.reshape(tp_count, moe_rows, column_list), "tp", 0, 0, tiled=True
    )
    attn_sum = jnp.sum(exchanged, axis=0)
    residual = (
        lax.dynamic_slice_in_dim(hidden_in, row_start, moe_rows, 0).astype(jnp.float32)
        + RESIDUAL * attn_sum
    )
    routed = normalize(residual).astype(jnp.bfloat16)
    experts = EXPERTS
    capacity = moe_rows // 2
    ff_part = expert_out.shape[1]
    onehot = (routes[:, :, None] == jnp.arange(experts, dtype=jnp.int32)[None, None, :]).astype(
        jnp.int32
    )
    per_row = jnp.sum(onehot, axis=1)
    before = jnp.cumsum(per_row, axis=0) - per_row
    rank_in = jnp.sum(onehot * before[:, None, :], axis=2)
    slot_of = routes * capacity + rank_in
    slot_ids = jnp.arange(experts * capacity, dtype=jnp.int32)
    pick_hit = slot_of[:, :, None] == slot_ids[None, None, :]
    selector = jnp.any(pick_hit, axis=1).T.astype(jnp.bfloat16)
    combiner = jnp.sum(jnp.where(pick_hit, gate_scores[:, :, None], 0.0), axis=1)
    gathered = jnp.dot(selector, routed, preferred_element_type=jnp.float32).astype(jnp.bfloat16)
    outgoing = gathered.reshape(experts, capacity, column_list)
    incoming = lax.all_to_all(outgoing, EXPERT_AXES, split_axis=0, concat_axis=0, tiled=True)
    incoming = incoming.reshape(experts * capacity, column_list)
    gate_up = jnp.einsum("rd,pdf->prf", incoming, full_in, preferred_element_type=jnp.float32)
    activated = (jax.nn.silu(gate_up[..., :ff_part]) * gate_up[..., ff_part:]).astype(jnp.bfloat16)
    partial_value = jnp.einsum(
        "prf,pfd->prd", activated, full_out, preferred_element_type=jnp.float32
    ).astype(jnp.bfloat16)
    part_total = jnp.sum(partial_value.astype(jnp.float32), axis=0).astype(jnp.bfloat16)
    returned = lax.all_to_all(
        part_total.reshape(experts, capacity, column_list), EXPERT_AXES, split_axis=0, concat_axis=0, tiled=True
    )
    part_sum = returned.reshape(experts * capacity, column_list).astype(jnp.float32)
    expert_sum = jnp.dot(
        combiner, part_sum, precision=lax.Precision.HIGHEST, preferred_element_type=jnp.float32
    )
    layer_out = (residual + RESIDUAL * expert_sum).astype(jnp.bfloat16)
    return (attn_sum.astype(jnp.bfloat16), expert_sum.astype(jnp.bfloat16), layer_out)


def solution(mesh):
    seq_size = mesh.shape["seq"]
    tp_size = mesh.shape["tp"]
    split = (seq_size // 16, 4, 2, 2, tp_size)
    fine_mesh = Mesh(mesh.devices.reshape(split), ("z", "yh", "yl", "c", "tp"))
    seq_spec = SEQ
    in_specs = (
        P(seq_spec, None),
        P(None, "tp"),
        P(None, "tp"),
        P(None, "tp"),
        P("tp", None),
        P(seq_spec, "tp"),
        P(seq_spec, "tp"),
        P(seq_spec, None),
        P(SEQ + ("tp",), None),
        P(SEQ + ("tp",), None),
        P(seq_spec, None, None),
        P(seq_spec, None, None),
    )
    out_specs = (P(SEQ + ("tp",), None),) * 3
    return jax.shard_map(body, mesh=fine_mesh, in_specs=in_specs, out_specs=out_specs, check_vma=False)
```

```python
import jax
import jax.numpy as jnp
from jax import lax
from jax.experimental import pallas as pl
from jax.sharding import Mesh, PartitionSpec as P

HEAD_WIDTH = 64
EXPERTS = 32


SEQ = ("z", "yh", "yl", "c")
EXPERT_AXES = ("z", "yh")
PART_AXES = ("yl", "c")
CHIP_AXES = ("z", "yh", "yl")
CORE_AXIS = "c"

EPSILON = 1e-06
RESIDUAL = 0.22


def normalize(values):
    values = values.astype(jnp.float32)
    return values * lax.rsqrt(jnp.mean(values * values, axis=-1, keepdims=True) + EPSILON)


def rotary_apply(values, token_positions):
    half_size = values.shape[-1] // 2
    frequency = jnp.exp(
        -jnp.log(10000.0) * jnp.arange(half_size, dtype=jnp.float32) * 2.0 / values.shape[-1]
    )
    angles = token_positions[:, None] * frequency[None, :]
    cosine = jnp.cos(angles)[:, None, :]
    sine_part = jnp.sin(angles)[:, None, :]
    first_half = values[..., :half_size]
    second = values[..., half_size:]
    return jnp.concatenate(
        [first_half * cosine - second * sine_part, second * cosine + first_half * sine_part],
        axis=-1,
    )


def prefix_attention(queries, keys_values, top_old, denom_old, numer_old, head_size):
    kv_local = queries.shape[0]
    value_base = keys_values.shape[1] // 2

    def kernel(q_ref, kv_ref, top_ref, den_ref, num_ref, out_ref):
        for head in range(kv_local):
            keys = kv_ref[:, head * head_size : (head + 1) * head_size]
            values = kv_ref[:, value_base + head * head_size : value_base + (head + 1) * head_size]
            scores = lax.dot_general(
                q_ref[head], keys, (((1,), (1,)), ((), ())), preferred_element_type=jnp.float32
            ) * (1.0 / head_size)
            top_prev = top_ref[head]
            top_new = jnp.maximum(top_prev, jnp.max(scores, axis=1, keepdims=True))
            shrink = jnp.exp(top_prev - top_new)
            weights = jnp.exp(scores - top_new)
            denom = den_ref[head] * shrink + jnp.sum(weights, axis=1, keepdims=True)
            numer = num_ref[head] * shrink + jnp.dot(
                weights.astype(jnp.bfloat16), values, preferred_element_type=jnp.float32
            )
            out_ref[head] = (numer / denom).astype(jnp.bfloat16)

    return pl.pallas_call(
        kernel, out_shape=jax.ShapeDtypeStruct(queries.shape, jnp.bfloat16)
    )(queries, keys_values, top_old, denom_old, numer_old)


def body(
    hidden_in,
    w_query,
    key_weight,
    value_weight,
    w_out,
    cached_prefix_keys,
    cached_prefix_values,
    doc_ids,
    routes,
    gate_scores,
    expert_in,
    expert_out,
):
    in_cols = expert_in.shape[2]
    packed = jnp.concatenate(
        [expert_in, expert_out.reshape(expert_out.shape[0], expert_in.shape[1], -1)], axis=2
    )
    packed = lax.all_gather(packed, PART_AXES, axis=0, tiled=True)
    full_in = packed[..., :in_cols]
    full_out = packed[..., in_cols:].reshape((packed.shape[0],) + expert_out.shape[1:])
    rows_dev = hidden_in.shape[0]
    column_list = hidden_in.shape[1]
    head_size = HEAD_WIDTH
    kv_local = key_weight.shape[1] // head_size
    group_width = w_query.shape[1] // head_size // kv_local
    seq_count = lax.axis_size(SEQ)
    prefix_len = cached_prefix_keys.shape[0] * seq_count
    doc_row = doc_ids[0]
    row_index = jnp.arange(rows_dev, dtype=jnp.int32)
    same_doc = doc_row[:, None] == doc_row[None, :]
    doc_start = jnp.min(jnp.where(same_doc, row_index[None, :], rows_dev), axis=1)
    token_positions = (prefix_len + row_index - doc_start).astype(jnp.float32)
    normed_input = normalize(hidden_in).astype(jnp.bfloat16)
    query_rows_all = jnp.dot(normed_input, w_query, preferred_element_type=jnp.float32).reshape(
        rows_dev, kv_local * group_width, head_size
    )
    query_rows_all = (
        rotary_apply(query_rows_all, token_positions)
        .astype(jnp.bfloat16)
        .reshape(rows_dev, kv_local, group_width, head_size)
    )
    fresh_key = jnp.dot(normed_input, key_weight, preferred_element_type=jnp.float32).reshape(
        rows_dev, kv_local, head_size
    )
    fresh_key = rotary_apply(fresh_key, token_positions).astype(jnp.bfloat16)
    fresh_value = (
        jnp.dot(normed_input, value_weight, preferred_element_type=jnp.float32)
        .astype(jnp.bfloat16)
        .reshape(rows_dev, kv_local, head_size)
    )
    own_scores = (
        jnp.einsum("tkgd,skd->tkgs", query_rows_all, fresh_key, preferred_element_type=jnp.float32)
        / head_size
    )
    visible = same_doc & (row_index[None, :] <= row_index[:, None])
    own_scores = jnp.where(visible[:, None, None, :], own_scores, -jnp.inf)
    row_top = jnp.max(own_scores, axis=-1)
    weights = jnp.exp(own_scores - row_top[..., None])
    denominator = jnp.sum(weights, axis=-1)
    numerator = jnp.einsum(
        "tkgs,skd->tkgd",
        weights.astype(jnp.bfloat16),
        fresh_value,
        preferred_element_type=jnp.float32,
    )
    running = (row_top, denominator, numerator)
    prefix_both = jnp.concatenate([cached_prefix_keys, cached_prefix_values], axis=1)
    chip_total = prefix_len // prefix_both.shape[0] // lax.axis_size(CORE_AXIS)
    same_core = lax.all_to_all(
        jnp.broadcast_to(prefix_both[None], (chip_total,) + prefix_both.shape), CHIP_AXES, 0, 0, tiled=True
    ).reshape(-1, prefix_both.shape[1])
    other_core = lax.ppermute(same_core, CORE_AXIS, [(0, 1), (1, 0)])
    whole_both = jnp.concatenate([same_core, other_core], axis=0)
    top_old, denom_old, numer_old = running
    rows_q = rows_dev * group_width

    def heads_first(values):
        return jnp.swapaxes(values, 0, 1).reshape((kv_local, rows_q) + values.shape[3:])

    attended = prefix_attention(
        heads_first(query_rows_all),
        whole_both,
        heads_first(top_old[..., None]),
        heads_first(denom_old[..., None]),
        heads_first(numer_old),
        head_size,
    )
    attended = jnp.swapaxes(
        attended.reshape(kv_local, rows_dev, group_width, head_size), 0, 1
    ).reshape(rows_dev, kv_local * group_width * head_size)
    moe_rows = routes.shape[0]
    row_start = lax.axis_index("tp") * moe_rows
    attn_part = jnp.dot(attended, w_out, preferred_element_type=jnp.float32)
    tp_count = lax.axis_size("tp")
    exchanged = lax.all_to_all(
        attn_part.astype(jnp.bfloat16).reshape(tp_count, moe_rows, column_list), "tp", 0, 0, tiled=True
    )
    attn_sum = jnp.sum(exchanged.astype(jnp.float32), axis=0)
    residual = (
        lax.dynamic_slice_in_dim(hidden_in, row_start, moe_rows, 0).astype(jnp.float32)
        + RESIDUAL * attn_sum
    )
    routed = normalize(residual).astype(jnp.bfloat16)
    experts = EXPERTS
    capacity = moe_rows // 2
    ff_part = expert_out.shape[1]
    onehot = (routes[:, :, None] == jnp.arange(experts, dtype=jnp.int32)[None, None, :]).astype(
        jnp.int32
    )
    per_row = jnp.sum(onehot, axis=1)
    before = jnp.cumsum(per_row, axis=0) - per_row
    rank_in = jnp.sum(onehot * before[:, None, :], axis=2)
    slot_of = routes * capacity + rank_in
    slot_ids = jnp.arange(experts * capacity, dtype=jnp.int32)
    pick_hit = slot_of[:, :, None] == slot_ids[None, None, :]
    selector = jnp.any(pick_hit, axis=1).T.astype(jnp.bfloat16)
    combiner = jnp.sum(jnp.where(pick_hit, gate_scores[:, :, None], 0.0), axis=1)
    gathered = jnp.dot(selector, routed, preferred_element_type=jnp.float32).astype(jnp.bfloat16)
    outgoing = gathered.reshape(experts, capacity, column_list)
    incoming = lax.all_to_all(outgoing, EXPERT_AXES, split_axis=0, concat_axis=0, tiled=True)
    incoming = incoming.reshape(experts * capacity, column_list)
    gate_up = jnp.einsum("rd,pdf->prf", incoming, full_in, preferred_element_type=jnp.float32)
    activated = (jax.nn.silu(gate_up[..., :ff_part]) * gate_up[..., ff_part:]).astype(jnp.bfloat16)
    partial_value = jnp.einsum(
        "prf,pfd->prd", activated, full_out, preferred_element_type=jnp.float32
    ).astype(jnp.bfloat16)
    part_total = jnp.sum(partial_value.astype(jnp.float32), axis=0).astype(jnp.bfloat16)
    returned = lax.all_to_all(
        part_total.reshape(experts, capacity, column_list), EXPERT_AXES, split_axis=0, concat_axis=0, tiled=True
    )
    part_sum = returned.reshape(experts * capacity, column_list).astype(jnp.float32)
    expert_sum = jnp.dot(
        combiner, part_sum, precision=lax.Precision.HIGHEST, preferred_element_type=jnp.float32
    )
    layer_out = (residual + RESIDUAL * expert_sum).astype(jnp.bfloat16)
    return (attn_sum.astype(jnp.bfloat16), expert_sum.astype(jnp.bfloat16), layer_out)


def solution(mesh):
    seq_size = mesh.shape["seq"]
    tp_size = mesh.shape["tp"]
    split = (seq_size // 16, 4, 2, 2, tp_size)
    fine_mesh = Mesh(mesh.devices.reshape(split), ("z", "yh", "yl", "c", "tp"))
    seq_spec = SEQ
    in_specs = (
        P(seq_spec, None),
        P(None, "tp"),
        P(None, "tp"),
        P(None, "tp"),
        P("tp", None),
        P(seq_spec, "tp"),
        P(seq_spec, "tp"),
        P(seq_spec, None),
        P(SEQ + ("tp",), None),
        P(SEQ + ("tp",), None),
        P(seq_spec, None, None),
        P(seq_spec, None, None),
    )
    out_specs = (P(SEQ + ("tp",), None),) * 3
    return jax.shard_map(body, mesh=fine_mesh, in_specs=in_specs, out_specs=out_specs, check_vma=False)
```
